128 devices in a mesh: slab: 32 (over z, y, x_hi), gy: 4 (over x_lo, core).
Axes of the slice: x: 4 (x_hi: 2, x_lo: 2; x = x_hi * 2 + x_lo), y: 4, z: 4, core: 2. Of those that a mesh axis runs over, the one named last changes fastest.
Arguments:
- electrostatic_voltages: float32 [256, 256, 1024], P('slab', 'gy'), may hold values from -6 to 6
- initial_electrons: float32 [256, 256, 1024], P('slab', 'gy'), may hold values from 0.5 to 2
- creation_amounts: float32 [256, 256, 1024], P('slab', 'gy'), may hold values from 0.2 to 5
- annihilation_coefficient: float32 [256, 256, 1024], P('slab', 'gy'), may hold values from 0.5 to 2
- crystal_orientation_class: int32 [256, 256, 1024], P('slab', 'gy'), may hold values from 0 to 3
- crystal_barrier_shift: float32 [4], replicated, may hold values from -1.5 to 1.5
- restrict_matrix_first: float32 [128, 256], replicated, may hold values from 0 to 1, as said below
- restrict_matrix_second: float32 [128, 64], P('gy'), may hold values from 0 to 1, as said below
- restrict_matrix_third: float32 [256, 1024], replicated, may hold values from 0 to 1, as said below
- cooling_coefficient: float32 [256, 128, 128], P('slab', 'gy'), may hold values from 0.05 to 1
- initial_warming: float32 [256, 128, 128], P('slab', 'gy'), may hold values from 0.5 to 1.5
Outputs:
- density_out: float32 [256, 256, 1024], P('slab', 'gy')
- thermal_out: float32 [256, 128, 128], P('slab', 'gy')
- fine_mesh_warming: float32 [256, 256, 1024], P('slab', 'gy')
The draws below stay inside these ranges and needn't reach their ends.
Inputs may be any that keep to these rules, and one draw needn't show every extreme that they name: `restrict_matrix_first`: row a is nonnegative, nonzero at most on columns 2a - 1 to 2a + 2, and sums to 1. `restrict_matrix_second`: row b, with t = b % 32, is nonnegative, nonzero at most on columns 2t - 1 to 2t + 2, and sums to 1. `restrict_matrix_third`: row c is nonnegative, nonzero at most on columns 4c - 2 to 4c + 5, and sums to 1.
All inputs are finite; a program needn't handle non-finite values.
Results may differ from the reference program's by a relative error of at most 0.0003.
Values sent between devices are 32-bit elements; how exact they have to be, the bound alone decides.
No kernel may reach another device: no remote copies, remote signals or barrier semaphores. Data moves between devices by JAX's collectives and lax.ppermute only.
A program may use at most 64 MiB of HBM per device.

```python
import math
import jax
import jax.numpy as jnp
from jax import lax

CY = 64
DEVICE_CELLS_Z = 1024
GRAINS = 4
SWEEPS = 2
HEAT_SWEEPS = 3
DEVICE_CELLS_X = 256
DEVICE_CELLS_Y = 256
HOT_MESH_ALONG_I = 128
TYD = 32
HOT_MESH_ALONG_J = 128
HOT_MESH_ALONG_K = 256
N_GY = 4


def banded_rows(key, local_rows, cols, ratio, taps):
    width = len(taps)
    shift = (width - ratio) // 2
    jitter = jax.random.uniform(key, (local_rows.shape[0], width), jnp.float32, 0.5, 1.5)
    column = jnp.arange(cols, dtype=jnp.int32)[None, :]
    start = (ratio * local_rows - shift)[:, None]
    matrix = jnp.zeros((local_rows.shape[0], cols), jnp.float32)
    for offset in range(width):
        matrix = matrix + jnp.where(column == start + offset, taps[offset] * jitter[:, offset:offset + 1], jnp.float32(0.0))
    return matrix / jnp.sum(matrix, axis=1, keepdims=True)


def draw_restrict_matrix_first(key, part):
    rows = jnp.arange(HOT_MESH_ALONG_I, dtype=jnp.int32)
    return banded_rows(jax.random.fold_in(key, 11), rows, DEVICE_CELLS_X, 2, [1.0, 3.0, 3.0, 1.0])


def draw_restrict_matrix_second(key, part):
    rows = jnp.arange(HOT_MESH_ALONG_J, dtype=jnp.int32) % TYD
    return banded_rows(jax.random.fold_in(key, 12), rows, CY, 2, [1.0, 3.0, 3.0, 1.0])


def draw_restrict_matrix_third(key, part):
    rows = jnp.arange(HOT_MESH_ALONG_K, dtype=jnp.int32)
    return banded_rows(jax.random.fold_in(key, 13), rows, DEVICE_CELLS_Z, 4, [1.0, 2.0, 3.0, 4.0, 4.0, 3.0, 2.0, 1.0])


def with_ends(entries, own_key, smallest, top_value):
    dims = entries.shape
    place = [jax.random.randint(jax.random.fold_in(own_key, axis), (), 0, dims[axis]) for axis in range(len(dims))]
    entries = entries.at[tuple(place)].set(smallest)
    longest = dims.index(max(dims))
    place[longest] = (place[longest] + 1) % dims[longest]
    return entries.at[tuple(place)].set(top_value)


def steps_of(stream_key, extent, split, low, high):
    level = 1.0
    for dim, parts in split:
        steps = jax.random.uniform(jax.random.fold_in(jax.random.fold_in(stream_key, 6), dim), (parts,), jnp.float32, low / len(split), high / len(split))
        level = level * jnp.repeat(jnp.exp(steps), extent[dim] // parts).reshape((-1,) + (1,) * (len(extent) - 1 - dim))
    return level


def scatter_about(key, extent, scale, most, split=(), held_as=jnp.bfloat16):
    factor_of = steps_of(key, extent, split, -0.22, 0.18) if split else 1.0
    values = jax.random.normal(key, extent, jnp.float32) * scale * factor_of
    return jnp.minimum(jnp.maximum(values, -most), most).astype(held_as)


def setup_inputs(seed: int = 0) -> dict:
    seeds = jax.random.split(jax.random.key(seed), 12)
    electrostatic_voltages = scatter_about(seeds[0], (DEVICE_CELLS_X, DEVICE_CELLS_Y, DEVICE_CELLS_Z), 1.0, 6.0, ((0, 32), (1, 4)), jnp.float32)
    initial_electrons = jnp.clip(jnp.exp(math.log(2.0) - 1.3862944 * jax.random.uniform(seeds[1], (DEVICE_CELLS_X, DEVICE_CELLS_Y, DEVICE_CELLS_Z), jnp.float32) ** steps_of(seeds[1], (DEVICE_CELLS_X, DEVICE_CELLS_Y, DEVICE_CELLS_Z), ((0, 32), (1, 4)), -0.2, 0.2)), 0.5, 2.0)
    creation_amounts = jnp.clip(jnp.exp(math.log(5.0) - 3.218876 * jax.random.uniform(seeds[2], (DEVICE_CELLS_X, DEVICE_CELLS_Y, DEVICE_CELLS_Z), jnp.float32) ** steps_of(seeds[2], (DEVICE_CELLS_X, DEVICE_CELLS_Y, DEVICE_CELLS_Z), ((0, 32), (1, 4)), -0.2, 0.2)), 0.2, 5.0)
    annihilation_coefficient = jnp.clip(jnp.exp(math.log(2.0) - 1.3862944 * jax.random.uniform(seeds[3], (DEVICE_CELLS_X, DEVICE_CELLS_Y, DEVICE_CELLS_Z), jnp.float32) ** steps_of(seeds[3], (DEVICE_CELLS_X, DEVICE_CELLS_Y, DEVICE_CELLS_Z), ((0, 32), (1, 4)), -0.2, 0.2)), 0.5, 2.0)
    crystal_orientation_class = with_ends(jax.random.randint(seeds[4], (DEVICE_CELLS_X, DEVICE_CELLS_Y, DEVICE_CELLS_Z), 0, GRAINS), jax.random.fold_in(seeds[4], 1), 0, GRAINS - 1).astype(jnp.int32)
    crystal_barrier_shift = jnp.clip(jax.random.uniform(seeds[5], (GRAINS,), jnp.float32, -1.5, 1.5), -1.5, 1.5)
    restrict_matrix_first = draw_restrict_matrix_first(jax.random.fold_in(seeds[11], 71), 0)
    restrict_matrix_second = draw_restrict_matrix_second(jax.random.fold_in(seeds[11], 71), 0)
    restrict_matrix_third = draw_restrict_matrix_third(jax.random.fold_in(seeds[11], 71), 0)
    cooling_coefficient = jnp.clip(jnp.exp(math.log(1.0) - 2.9957323 * jax.random.uniform(seeds[9], (HOT_MESH_ALONG_K, HOT_MESH_ALONG_J, HOT_MESH_ALONG_I), jnp.float32) ** steps_of(seeds[9], (HOT_MESH_ALONG_K, HOT_MESH_ALONG_J, HOT_MESH_ALONG_I), ((0, 32), (1, 4)), -0.2, 0.2)), 0.05, 1.0)
    initial_warming = jnp.clip(0.5 + 1.0 * jax.random.uniform(seeds[10], (HOT_MESH_ALONG_K, HOT_MESH_ALONG_J, HOT_MESH_ALONG_I), jnp.float32) ** steps_of(seeds[10], (HOT_MESH_ALONG_K, HOT_MESH_ALONG_J, HOT_MESH_ALONG_I), ((0, 32), (1, 4)), -0.2, 0.2), 0.5, 1.5)
    return dict(electrostatic_voltages=electrostatic_voltages, initial_electrons=initial_electrons, creation_amounts=creation_amounts, annihilation_coefficient=annihilation_coefficient, crystal_orientation_class=crystal_orientation_class, crystal_barrier_shift=crystal_barrier_shift, restrict_matrix_first=restrict_matrix_first, restrict_matrix_second=restrict_matrix_second, restrict_matrix_third=restrict_matrix_third, cooling_coefficient=cooling_coefficient, initial_warming=initial_warming)


def bernoulli(value):
    small = jnp.abs(value) < 1e-4
    safe = jnp.where(small, jnp.float32(1.0), value)
    return jnp.where(small, 1.0 - 0.5 * value, safe / jnp.expm1(safe))


def neighbour_values(padded):
    return [padded[2:, 1:-1, 1:-1], padded[:-2, 1:-1, 1:-1], padded[1:-1, 2:, 1:-1], padded[1:-1, :-2, 1:-1], padded[1:-1, 1:-1, 2:], padded[1:-1, 1:-1, :-2]]


def reference(electrostatic_voltages, initial_electrons, creation_amounts, annihilation_coefficient, crystal_orientation_class, crystal_barrier_shift, restrict_matrix_first, restrict_matrix_second, restrict_matrix_third, cooling_coefficient, initial_warming):
    upper_limit = lax.Precision.HIGHEST
    effective = electrostatic_voltages
    for grain in range(GRAINS):
        effective = effective + jnp.where(crystal_orientation_class == grain, crystal_barrier_shift[grain], jnp.float32(0.0))
    beside_all = neighbour_values(jnp.pad(effective, 1))
    voltage_gradients = [leftover_portion - effective for leftover_portion in beside_all]
    bernoulli_coefficients = [bernoulli(voltage_gradient) for voltage_gradient in voltage_gradients]
    denominator_quantity = annihilation_coefficient
    for bernoulli_coefficient, voltage_gradient in zip(bernoulli_coefficients, voltage_gradients):
        denominator_quantity = denominator_quantity + (bernoulli_coefficient + voltage_gradient)
    electron_concentration = initial_electrons
    for repeat in range(SWEEPS):
        fraction_top_quantity = creation_amounts
        for bernoulli_coefficient, leftover_portion in zip(bernoulli_coefficients, neighbour_values(jnp.pad(electron_concentration, 1))):
            fraction_top_quantity = fraction_top_quantity + bernoulli_coefficient * leftover_portion
        electron_concentration = fraction_top_quantity / denominator_quantity
    joule_power_input = jnp.zeros_like(electron_concentration)
    for bernoulli_coefficient, voltage_gradient, leftover_portion in zip(bernoulli_coefficients, voltage_gradients, neighbour_values(jnp.pad(electron_concentration, 1))):
        joule_power_input = joule_power_input + voltage_gradient * (bernoulli_coefficient * leftover_portion - (bernoulli_coefficient + voltage_gradient) * electron_concentration)
    joule_power_input = 0.5 * joule_power_input
    y_block_count = restrict_matrix_second.reshape(N_GY, TYD, CY)
    along_y = jnp.einsum('gty,xgyz->xgtz', y_block_count, joule_power_input.reshape(DEVICE_CELLS_X, N_GY, CY, DEVICE_CELLS_Z), precision=upper_limit).reshape(DEVICE_CELLS_X, HOT_MESH_ALONG_J, DEVICE_CELLS_Z)
    along_z = jnp.einsum('cz,xtz->ctx', restrict_matrix_third, along_y, precision=upper_limit)
    source = jnp.einsum('ctx,ax->cta', along_z, restrict_matrix_first, precision=upper_limit)
    warming_distribution = initial_warming
    for repeat in range(HEAT_SWEEPS):
        total = source
        for leftover_portion in neighbour_values(jnp.pad(warming_distribution, 1)):
            total = total + leftover_portion
        warming_distribution = total / (6.0 + cooling_coefficient)
    spread = jnp.einsum('cta,ax->ctx', warming_distribution, restrict_matrix_first, precision=upper_limit)
    raised_field = jnp.einsum('ctx,cz->xtz', spread, restrict_matrix_third, precision=upper_limit).reshape(DEVICE_CELLS_X, N_GY, TYD, DEVICE_CELLS_Z)
    fine_mesh_warming = 16.0 * jnp.einsum('efc,iefk->ieck', y_block_count, raised_field, precision=upper_limit).reshape(DEVICE_CELLS_X, DEVICE_CELLS_Y, DEVICE_CELLS_Z)
    return electron_concentration, warming_distribution, fine_mesh_warming
```

```python
import jax
import jax.numpy as jnp
from jax import lax
from jax.sharding import PartitionSpec as P

GRAINS = 4
HEAT_SWEEPS = 3
BAND = 6


def face_halos(block, sides):
    halos = []
    for axis, dim in sides:
        count = lax.axis_size(axis)
        forward = [(i, i + 1) for i in range(count - 1)]
        backward = [(i + 1, i) for i in range(count - 1)]
        size = block.shape[dim]
        low = lax.ppermute(lax.slice_in_dim(block, size - 1, size, axis=dim), axis, forward)
        high = lax.ppermute(lax.slice_in_dim(block, 0, 1, axis=dim), axis, backward)
        halos.append((low, high))
    return halos


def neighbours_of(block, halos, lead=0):
    out = []
    for k, (low, high) in enumerate(halos):
        dim = lead + k
        size = block.shape[dim]
        out.append(jnp.concatenate([lax.slice_in_dim(block, 1, size, axis=dim), high], axis=dim))
        out.append(jnp.concatenate([low, lax.slice_in_dim(block, 0, size - 1, axis=dim)], axis=dim))
    last = block.ndim - 1
    size = block.shape[last]
    zero = jnp.zeros_like(lax.slice_in_dim(block, 0, 1, axis=last))
    out.append(jnp.concatenate([lax.slice_in_dim(block, 1, size, axis=last), zero], axis=last))
    out.append(jnp.concatenate([zero, lax.slice_in_dim(block, 0, size - 1, axis=last)], axis=last))
    return out


def bernoulli(value):
    small = jnp.abs(value) < 0.0001
    safe = jnp.where(small, jnp.float32(1.0), value)
    return jnp.where(small, 1.0 - 0.5 * value, safe / jnp.expm1(safe))


def per_device(
    electrostatic_voltages,
    initial_electrons,
    creation_amounts,
    annihilation_coefficient,
    crystal_orientation_class,
    crystal_barrier_shift,
    restrict_matrix_first,
    restrict_matrix_second,
    restrict_matrix_third,
    cooling_coefficient,
    initial_warming,
):
    upper_limit = lax.Precision.HIGHEST
    slab_cells = electrostatic_voltages.shape[0]
    slabs = lax.axis_size("slab")
    me = lax.axis_index("slab")
    effective = electrostatic_voltages
    for grain in range(GRAINS):
        effective = effective + jnp.where(
            crystal_orientation_class == grain, crystal_barrier_shift[grain], jnp.float32(0.0)
        )
    device_sides = (("slab", 0), ("gy", 1))
    both = jnp.stack([effective, initial_electrons])
    both_halos = face_halos(both, (("slab", 1), ("gy", 2)))
    beside_both = neighbours_of(both, both_halos, lead=1)
    beside_all = [b[0] for b in beside_both]
    voltage_gradients = [leftover_portion - effective for leftover_portion in beside_all]
    bernoulli_coefficients = [bernoulli(voltage_gradient) for voltage_gradient in voltage_gradients]
    denominator_quantity = annihilation_coefficient
    for bernoulli_coefficient, voltage_gradient in zip(bernoulli_coefficients, voltage_gradients):
        denominator_quantity = denominator_quantity + (bernoulli_coefficient + voltage_gradient)

    def sweep(beside):
        fraction_top_quantity = creation_amounts
        for bernoulli_coefficient, leftover_portion in zip(bernoulli_coefficients, beside):
            fraction_top_quantity = fraction_top_quantity + bernoulli_coefficient * leftover_portion
        return fraction_top_quantity / denominator_quantity

    electron_concentration = sweep([b[1] for b in beside_both])
    electron_concentration = sweep(
        neighbours_of(electron_concentration, face_halos(electron_concentration, device_sides))
    )
    beside_final = neighbours_of(
        electron_concentration, face_halos(electron_concentration, device_sides)
    )
    joule_power_input = jnp.zeros_like(electron_concentration)
    for bernoulli_coefficient, voltage_gradient, leftover_portion in zip(
        bernoulli_coefficients, voltage_gradients, beside_final
    ):
        joule_power_input = joule_power_input + voltage_gradient * (
            bernoulli_coefficient * leftover_portion
            - (bernoulli_coefficient + voltage_gradient) * electron_concentration
        )
    joule_power_input = 0.5 * joule_power_input

    padded_first = jnp.pad(restrict_matrix_first, ((1, 1), (0, 0)))
    ratio = slab_cells // 2
    columns = lax.dynamic_slice(
        padded_first, (me * ratio, me * slab_cells), (BAND, slab_cells)
    )
    along_y = jnp.einsum(
        "ty,xyz->xtz", restrict_matrix_second, joule_power_input, precision=upper_limit
    )
    along_z = jnp.einsum("cz,xtz->ctx", restrict_matrix_third, along_y, precision=upper_limit)
    piece = jnp.einsum("ctx,ax->cta", along_z, columns, precision=upper_limit)
    chunk_c = piece.shape[0] // slabs
    piece = piece.reshape(slabs, chunk_c, piece.shape[1], BAND)
    got = lax.all_to_all(piece, "slab", 0, 0, tiled=False)
    main = got[..., 1 : 1 + ratio]
    zero_row = jnp.zeros_like(got[:1, ..., 0])
    left = jnp.concatenate([got[1:, ..., 0], zero_row], axis=0)
    right = jnp.concatenate([zero_row, got[:-1, ..., ratio + 1]], axis=0)
    main = main.at[..., ratio - 1].add(left)
    main = main.at[..., 0].add(right)
    source = jnp.transpose(main, (1, 2, 0, 3)).reshape(chunk_c, main.shape[2], slabs * ratio)

    warming_distribution = initial_warming
    thermal_sides = (("slab", 0), ("gy", 1))
    for repeat in range(HEAT_SWEEPS):
        beside = neighbours_of(
            warming_distribution, face_halos(warming_distribution, thermal_sides)
        )
        total = source
        for leftover_portion in beside:
            total = total + leftover_portion
        warming_distribution = total / (6.0 + cooling_coefficient)

    padded_warm = jnp.pad(warming_distribution, ((0, 0), (0, 0), (1, 1)))
    windows = jnp.stack(
        [padded_warm[..., ratio * s : ratio * s + BAND] for s in range(slabs)]
    )
    got_warm = lax.all_to_all(windows, "slab", 0, 0, tiled=False)
    got_warm = got_warm.reshape(slabs * chunk_c, got_warm.shape[2], BAND)
    spread = jnp.einsum("cta,ax->ctx", got_warm, columns, precision=upper_limit)
    raised_field = jnp.einsum(
        "ctx,cz->xtz", spread, restrict_matrix_third, precision=upper_limit
    )
    fine_mesh_warming = 16.0 * jnp.einsum(
        "hc,qhk->qck", restrict_matrix_second, raised_field, precision=upper_limit
    )
    return (electron_concentration, warming_distribution, fine_mesh_warming)


def solution(mesh):
    in_specs = (
        P("slab", "gy", None),
        P("slab", "gy", None),
        P("slab", "gy", None),
        P("slab", "gy", None),
        P("slab", "gy", None),
        P(),
        P(),
        P("gy", None),
        P(),
        P("slab", "gy", None),
        P("slab", "gy", None),
    )
    out_specs = (P("slab", "gy", None), P("slab", "gy", None), P("slab", "gy", None))
    return jax.shard_map(
        per_device, mesh=mesh, in_specs=in_specs, out_specs=out_specs, check_vma=False
    )
```

```python
import jax
import jax.numpy as jnp
from jax import lax
from jax.sharding import PartitionSpec as P

GRAINS = 4
HEAT_SWEEPS = 3
BAND = 6


def face_halos(block, sides):
    halos = []
    for axis, dim in sides:
        count = lax.axis_size(axis)
        forward = [(i, i + 1) for i in range(count - 1)]
        backward = [(i + 1, i) for i in range(count - 1)]
        size = block.shape[dim]
        low = lax.ppermute(lax.slice_in_dim(block, size - 1, size, axis=dim), axis, forward)
        high = lax.ppermute(lax.slice_in_dim(block, 0, 1, axis=dim), axis, backward)
        halos.append((low, high))
    return halos


def neighbours_of(block, halos, lead=0):
    out = []
    for k, (low, high) in enumerate(halos):
        dim = lead + k
        size = block.shape[dim]
        out.append(jnp.concatenate([lax.slice_in_dim(block, 1, size, axis=dim), high], axis=dim))
        out.append(jnp.concatenate([low, lax.slice_in_dim(block, 0, size - 1, axis=dim)], axis=dim))
    last = block.ndim - 1
    size = block.shape[last]
    zero = jnp.zeros_like(lax.slice_in_dim(block, 0, 1, axis=last))
    out.append(jnp.concatenate([lax.slice_in_dim(block, 1, size, axis=last), zero], axis=last))
    out.append(jnp.concatenate([zero, lax.slice_in_dim(block, 0, size - 1, axis=last)], axis=last))
    return out


def bernoulli(value):
    small = jnp.abs(value) < 0.0001
    safe = jnp.where(small, jnp.float32(1.0), value)
    return jnp.where(small, 1.0 - 0.5 * value, safe / jnp.expm1(safe))


def per_device(
    electrostatic_voltages,
    initial_electrons,
    creation_amounts,
    annihilation_coefficient,
    crystal_orientation_class,
    crystal_barrier_shift,
    restrict_matrix_first,
    restrict_matrix_second,
    restrict_matrix_third,
    cooling_coefficient,
    initial_warming,
):
    upper_limit = lax.Precision.HIGHEST
    slab_cells = electrostatic_voltages.shape[0]
    slabs = lax.axis_size("slab")
    me = lax.axis_index("slab")
    effective = electrostatic_voltages
    for grain in range(GRAINS):
        effective = effective + jnp.where(
            crystal_orientation_class == grain, crystal_barrier_shift[grain], jnp.float32(0.0)
        )
    device_sides = (("slab", 0), ("gy", 1))
    both = jnp.stack([effective, initial_electrons])
    both_halos = face_halos(both, (("slab", 1), ("gy", 2)))
    beside_both = neighbours_of(both, both_halos, lead=1)
    beside_all = [b[0] for b in beside_both]
    voltage_gradients = [leftover_portion - effective for leftover_portion in beside_all]
    bernoulli_coefficients = [bernoulli(voltage_gradient) for voltage_gradient in voltage_gradients]
    denominator_quantity = annihilation_coefficient
    for bernoulli_coefficient, voltage_gradient in zip(bernoulli_coefficients, voltage_gradients):
        denominator_quantity = denominator_quantity + (bernoulli_coefficient + voltage_gradient)

    def sweep(beside):
        fraction_top_quantity = creation_amounts
        for bernoulli_coefficient, leftover_portion in zip(bernoulli_coefficients, beside):
            fraction_top_quantity = fraction_top_quantity + bernoulli_coefficient * leftover_portion
        return fraction_top_quantity / denominator_quantity

    electron_concentration = sweep([b[1] for b in beside_both])
    electron_concentration = sweep(
        neighbours_of(electron_concentration, face_halos(electron_concentration, device_sides))
    )
    n_final = electron_concentration
    y_low, y_high = face_halos(n_final, (("gy", 1),))[0]
    zero_x = jnp.zeros_like(n_final[:1])
    beside_final = neighbours_of(n_final, [(zero_x, zero_x), (y_low, y_high)])
    joule_power_input = jnp.zeros_like(n_final)
    for bernoulli_coefficient, voltage_gradient, leftover_portion in zip(
        bernoulli_coefficients, voltage_gradients, beside_final
    ):
        joule_power_input = joule_power_input + voltage_gradient * (
            bernoulli_coefficient * leftover_portion
            - (bernoulli_coefficient + voltage_gradient) * n_final
        )
    joule_power_input = 0.5 * joule_power_input
    up_x, down_x = voltage_gradients[0], voltage_gradients[1]
    bup_x, bdown_x = bernoulli_coefficients[0], bernoulli_coefficients[1]
    heat_left = -0.5 * (down_x[:1] * ((bdown_x[:1] + down_x[:1]) * n_final[:1]))
    heat_right = -0.5 * (up_x[-1:] * ((bup_x[-1:] + up_x[-1:]) * n_final[-1:]))
    heat_ext = jnp.concatenate([heat_left, joule_power_input, heat_right], axis=0)

    padded_first = jnp.pad(restrict_matrix_first, ((1, 1), (1, 1)))
    ratio = slab_cells // 2
    columns_ext = lax.dynamic_slice(
        padded_first, (me * ratio, me * slab_cells), (BAND, slab_cells + 2)
    )
    columns = columns_ext[:, 1 : 1 + slab_cells]
    along_y = jnp.einsum(
        "ty,xyz->xtz", restrict_matrix_second, heat_ext, precision=upper_limit
    )
    along_z = jnp.einsum("cz,xtz->ctx", restrict_matrix_third, along_y, precision=upper_limit)
    piece = jnp.einsum("ctx,ax->cta", along_z, columns_ext, precision=upper_limit)
    chunk_c = piece.shape[0] // slabs
    piece = piece.reshape(slabs, chunk_c, piece.shape[1], BAND)
    got = lax.all_to_all(piece, "slab", 0, 0, tiled=False)
    main = got[..., 1 : 1 + ratio]
    zero_row = jnp.zeros_like(got[:1, ..., 0])
    left = jnp.concatenate([got[1:, ..., 0], zero_row], axis=0)
    right = jnp.concatenate([zero_row, got[:-1, ..., ratio + 1]], axis=0)
    main = main.at[..., ratio - 1].add(left)
    main = main.at[..., 0].add(right)
    source = jnp.transpose(main, (1, 2, 0, 3)).reshape(chunk_c, main.shape[2], slabs * ratio)

    depth = HEAT_SWEEPS
    stacked = jnp.stack([initial_warming, source, 6.0 + cooling_coefficient])
    for axis, dim in (("slab", 1), ("gy", 2)):
        count = lax.axis_size(axis)
        forward = [(i, i + 1) for i in range(count - 1)]
        backward = [(i + 1, i) for i in range(count - 1)]
        size = stacked.shape[dim]
        low = lax.ppermute(lax.slice_in_dim(stacked, size - depth, size, axis=dim), axis, forward)
        high = lax.ppermute(lax.slice_in_dim(stacked, 0, depth, axis=dim), axis, backward)
        stacked = jnp.concatenate([low, stacked, high], axis=dim)
    tc, tb = initial_warming.shape[0], initial_warming.shape[1]
    c_index = lax.broadcasted_iota(jnp.int32, stacked.shape[1:], 0) + (me * tc - depth)
    b_index = lax.broadcasted_iota(jnp.int32, stacked.shape[1:], 1) + (
        lax.axis_index("gy") * tb - depth
    )
    inside = (
        (c_index >= 0)
        & (c_index < slabs * tc)
        & (b_index >= 0)
        & (b_index < lax.axis_size("gy") * tb)
    )
    warm = stacked[0]
    for repeat in range(HEAT_SWEEPS):
        r = repeat + 1
        ce, be = warm.shape[0] - 2, warm.shape[1] - 2
        zero_a = jnp.zeros_like(warm[1:-1, 1:-1, :1])
        core = warm[1:-1, 1:-1]
        total = stacked[1, r : r + ce, r : r + be]
        for leftover_portion in (
            warm[2:, 1:-1],
            warm[:-2, 1:-1],
            warm[1:-1, 2:],
            warm[1:-1, :-2],
            jnp.concatenate([core[..., 1:], zero_a], axis=2),
            jnp.concatenate([zero_a, core[..., :-1]], axis=2),
        ):
            total = total + leftover_portion
        warm = jnp.where(
            inside[r : r + ce, r : r + be], total / stacked[2, r : r + ce, r : r + be], 0.0
        )
    warming_distribution = warm

    padded_warm = jnp.pad(warming_distribution, ((0, 0), (0, 0), (1, 1)))
    windows = jnp.stack(
        [padded_warm[..., ratio * s : ratio * s + BAND] for s in range(slabs)]
    )
    got_warm = lax.all_to_all(windows, "slab", 0, 0, tiled=False)
    got_warm = got_warm.reshape(slabs * chunk_c, got_warm.shape[2], BAND)
    spread = jnp.einsum("cta,ax->ctx", got_warm, columns, precision=upper_limit)
    raised_field = jnp.einsum(
        "ctx,cz->xtz", spread, restrict_matrix_third, precision=upper_limit
    )
    fine_mesh_warming = 16.0 * jnp.einsum(
        "hc,qhk->qck", restrict_matrix_second, raised_field, precision=upper_limit
    )
    return (electron_concentration, warming_distribution, fine_mesh_warming)


def solution(mesh):
    in_specs = (
        P("slab", "gy", None),
        P("slab", "gy", None),
        P("slab", "gy", None),
        P("slab", "gy", None),
        P("slab", "gy", None),
        P(),
        P(),
        P("gy", None),
        P(),
        P("slab", "gy", None),
        P("slab", "gy", None),
    )
    out_specs = (P("slab", "gy", None), P("slab", "gy", None), P("slab", "gy", None))
    return jax.shard_map(
        per_device, mesh=mesh, in_specs=in_specs, out_specs=out_specs, check_vma=False
    )
```

```python
import jax
import jax.numpy as jnp
from jax import lax
from jax.sharding import PartitionSpec as P

GRAINS = 4
HEAT_SWEEPS = 3
BAND = 6


def face_halos(block, sides):
    halos = []
    for axis, dim in sides:
        count = lax.axis_size(axis)
        forward = [(i, i + 1) for i in range(count - 1)]
        backward = [(i + 1, i) for i in range(count - 1)]
        size = block.shape[dim]
        low = lax.ppermute(lax.slice_in_dim(block, size - 1, size, axis=dim), axis, forward)
        high = lax.ppermute(lax.slice_in_dim(block, 0, 1, axis=dim), axis, backward)
        halos.append((low, high))
    return halos


def face_halos_of(blocks, sides):
    halos = [[] for _ in blocks]
    for axis, dim in sides:
        count = lax.axis_size(axis)
        forward = [(i, i + 1) for i in range(count - 1)]
        backward = [(i + 1, i) for i in range(count - 1)]
        size = blocks[0].shape[dim]
        low = lax.ppermute(
            jnp.stack([lax.slice_in_dim(b, size - 1, size, axis=dim) for b in blocks]),
            axis,
            forward,
        )
        high = lax.ppermute(
            jnp.stack([lax.slice_in_dim(b, 0, 1, axis=dim) for b in blocks]), axis, backward
        )
        for k in range(len(blocks)):
            halos[k].append((low[k], high[k]))
    return halos


def neighbours_of(block, halos, lead=0):
    out = []
    for k, (low, high) in enumerate(halos):
        dim = lead + k
        size = block.shape[dim]
        out.append(jnp.concatenate([lax.slice_in_dim(block, 1, size, axis=dim), high], axis=dim))
        out.append(jnp.concatenate([low, lax.slice_in_dim(block, 0, size - 1, axis=dim)], axis=dim))
    last = block.ndim - 1
    size = block.shape[last]
    zero = jnp.zeros_like(lax.slice_in_dim(block, 0, 1, axis=last))
    out.append(jnp.concatenate([lax.slice_in_dim(block, 1, size, axis=last), zero], axis=last))
    out.append(jnp.concatenate([zero, lax.slice_in_dim(block, 0, size - 1, axis=last)], axis=last))
    return out


def bernoulli(value):
    small = jnp.abs(value) < 0.0001
    safe = jnp.where(small, jnp.float32(1.0), value)
    return jnp.where(small, 1.0 - 0.5 * value, safe / jnp.expm1(safe))


def per_device(
    electrostatic_voltages,
    initial_electrons,
    creation_amounts,
    annihilation_coefficient,
    crystal_orientation_class,
    crystal_barrier_shift,
    restrict_matrix_first,
    restrict_matrix_second,
    restrict_matrix_third,
    cooling_coefficient,
    initial_warming,
):
    upper_limit = lax.Precision.HIGHEST
    slab_cells = electrostatic_voltages.shape[0]
    slabs = lax.axis_size("slab")
    me = lax.axis_index("slab")
    effective = electrostatic_voltages
    for grain in range(GRAINS):
        effective = effective + jnp.where(
            crystal_orientation_class == grain, crystal_barrier_shift[grain], jnp.float32(0.0)
        )
    device_sides = (("slab", 0), ("gy", 1))
    eff_halos, start_halos = face_halos_of([effective, initial_electrons], device_sides)
    beside_all = neighbours_of(effective, eff_halos)
    voltage_gradients = [leftover_portion - effective for leftover_portion in beside_all]
    up_coefficients = lax.optimization_barrier(
        tuple(bernoulli(voltage_gradients[d]) for d in (0, 2, 4))
    )
    bernoulli_coefficients = []
    for k, dim in enumerate((0, 1, 2)):
        up_b, up_u, down_u = up_coefficients[k], voltage_gradients[2 * k], voltage_gradients[2 * k + 1]
        size = up_b.shape[dim]
        first = bernoulli(lax.slice_in_dim(down_u, 0, 1, axis=dim))
        rest = lax.slice_in_dim(up_b + up_u, 0, size - 1, axis=dim)
        bernoulli_coefficients += [up_b, jnp.concatenate([first, rest], axis=dim)]
    denominator_quantity = annihilation_coefficient
    for bernoulli_coefficient, voltage_gradient in zip(bernoulli_coefficients, voltage_gradients):
        denominator_quantity = denominator_quantity + (bernoulli_coefficient + voltage_gradient)

    def sweep(beside):
        fraction_top_quantity = creation_amounts
        for bernoulli_coefficient, leftover_portion in zip(bernoulli_coefficients, beside):
            fraction_top_quantity = fraction_top_quantity + bernoulli_coefficient * leftover_portion
        return fraction_top_quantity / denominator_quantity

    electron_concentration = sweep(neighbours_of(initial_electrons, start_halos))
    electron_concentration = sweep(
        neighbours_of(electron_concentration, face_halos(electron_concentration, device_sides))
    )
    n_final = electron_concentration
    y_low, y_high = face_halos(n_final, (("gy", 1),))[0]
    zero_x = jnp.zeros_like(n_final[:1])
    beside_final = neighbours_of(n_final, [(zero_x, zero_x), (y_low, y_high)])
    joule_power_input = jnp.zeros_like(n_final)
    for bernoulli_coefficient, voltage_gradient, leftover_portion in zip(
        bernoulli_coefficients, voltage_gradients, beside_final
    ):
        joule_power_input = joule_power_input + voltage_gradient * (
            bernoulli_coefficient * leftover_portion
            - (bernoulli_coefficient + voltage_gradient) * n_final
        )
    joule_power_input = 0.5 * joule_power_input
    up_x, down_x = voltage_gradients[0], voltage_gradients[1]
    bup_x, bdown_x = bernoulli_coefficients[0], bernoulli_coefficients[1]
    heat_left = -0.5 * (down_x[:1] * ((bdown_x[:1] + down_x[:1]) * n_final[:1]))
    heat_right = -0.5 * (up_x[-1:] * ((bup_x[-1:] + up_x[-1:]) * n_final[-1:]))
    heat_ext = jnp.concatenate([heat_left, joule_power_input, heat_right], axis=0)

    padded_first = jnp.pad(restrict_matrix_first, ((1, 1), (1, 1)))
    ratio = slab_cells // 2
    columns_ext = lax.dynamic_slice(
        padded_first, (me * ratio, me * slab_cells), (BAND, slab_cells + 2)
    )
    columns = columns_ext[:, 1 : 1 + slab_cells]
    along_y = jnp.einsum(
        "ty,xyz->xtz", restrict_matrix_second, heat_ext, precision=upper_limit
    )
    along_z = jnp.einsum("cz,xtz->ctx", restrict_matrix_third, along_y, precision=upper_limit)
    piece = jnp.einsum("ctx,ax->cta", along_z, columns_ext, precision=upper_limit)
    chunk_c = piece.shape[0] // slabs
    piece = piece.reshape(slabs, chunk_c, piece.shape[1], BAND)
    got = lax.all_to_all(piece, "slab", 0, 0, tiled=False)
    main = got[..., 1 : 1 + ratio]
    zero_row = jnp.zeros_like(got[:1, ..., 0])
    left = jnp.concatenate([got[1:, ..., 0], zero_row], axis=0)
    right = jnp.concatenate([zero_row, got[:-1, ..., ratio + 1]], axis=0)
    main = main.at[..., ratio - 1].add(left)
    main = main.at[..., 0].add(right)
    source = jnp.transpose(main, (1, 2, 0, 3)).reshape(chunk_c, main.shape[2], slabs * ratio)

    depth = HEAT_SWEEPS
    stacked = jnp.stack([initial_warming, source, 6.0 + cooling_coefficient])
    for axis, dim in (("slab", 1), ("gy", 2)):
        count = lax.axis_size(axis)
        forward = [(i, i + 1) for i in range(count - 1)]
        backward = [(i + 1, i) for i in range(count - 1)]
        size = stacked.shape[dim]
        low = lax.ppermute(lax.slice_in_dim(stacked, size - depth, size, axis=dim), axis, forward)
        high = lax.ppermute(lax.slice_in_dim(stacked, 0, depth, axis=dim), axis, backward)
        stacked = jnp.concatenate([low, stacked, high], axis=dim)
    tc, tb = initial_warming.shape[0], initial_warming.shape[1]
    c_index = lax.broadcasted_iota(jnp.int32, stacked.shape[1:], 0) + (me * tc - depth)
    b_index = lax.broadcasted_iota(jnp.int32, stacked.shape[1:], 1) + (
        lax.axis_index("gy") * tb - depth
    )
    inside = (
        (c_index >= 0)
        & (c_index < slabs * tc)
        & (b_index >= 0)
        & (b_index < lax.axis_size("gy") * tb)
    )
    warm = stacked[0]
    for repeat in range(HEAT_SWEEPS):
        r = repeat + 1
        ce, be = warm.shape[0] - 2, warm.shape[1] - 2
        zero_a = jnp.zeros_like(warm[1:-1, 1:-1, :1])
        core = warm[1:-1, 1:-1]
        total = stacked[1, r : r + ce, r : r + be]
        for leftover_portion in (
            warm[2:, 1:-1],
            warm[:-2, 1:-1],
            warm[1:-1, 2:],
            warm[1:-1, :-2],
            jnp.concatenate([core[..., 1:], zero_a], axis=2),
            jnp.concatenate([zero_a, core[..., :-1]], axis=2),
        ):
            total = total + leftover_portion
        warm = jnp.where(
            inside[r : r + ce, r : r + be], total / stacked[2, r : r + ce, r : r + be], 0.0
        )
    warming_distribution = warm

    padded_warm = jnp.pad(warming_distribution, ((0, 0), (0, 0), (1, 1)))
    windows = jnp.stack(
        [padded_warm[..., ratio * s : ratio * s + BAND] for s in range(slabs)]
    )
    got_warm = lax.all_to_all(windows, "slab", 0, 0, tiled=False)
    got_warm = got_warm.reshape(slabs * chunk_c, got_warm.shape[2], BAND)
    spread = jnp.einsum("cta,ax->ctx", got_warm, columns, precision=upper_limit)
    raised_field = jnp.einsum(
        "ctx,cz->xtz", spread, restrict_matrix_third, precision=upper_limit
    )
    fine_mesh_warming = 16.0 * jnp.einsum(
        "hc,qhk->qck", restrict_matrix_second, raised_field, precision=upper_limit
    )
    return (electron_concentration, warming_distribution, fine_mesh_warming)


def solution(mesh):
    in_specs = (
        P("slab", "gy", None),
        P("slab", "gy", None),
        P("slab", "gy", None),
        P("slab", "gy", None),
        P("slab", "gy", None),
        P(),
        P(),
        P("gy", None),
        P(),
        P("slab", "gy", None),
        P("slab", "gy", None),
    )
    out_specs = (P("slab", "gy", None), P("slab", "gy", None), P("slab", "gy", None))
    return jax.shard_map(
        per_device, mesh=mesh, in_specs=in_specs, out_specs=out_specs, check_vma=False
    )
```

```python
import jax
import jax.numpy as jnp
from jax import lax
from jax.sharding import PartitionSpec as P

GRAINS = 4
HEAT_SWEEPS = 3
BAND = 6


def face_halos(block, sides):
    halos = []
    for axis, dim in sides:
        count = lax.axis_size(axis)
        forward = [(i, i + 1) for i in range(count - 1)]
        backward = [(i + 1, i) for i in range(count - 1)]
        size = block.shape[dim]
        low = lax.ppermute(lax.slice_in_dim(block, size - 1, size, axis=dim), axis, forward)
        high = lax.ppermute(lax.slice_in_dim(block, 0, 1, axis=dim), axis, backward)
        halos.append((low, high))
    return halos


def neighbours_of(block, halos, lead=0):
    out = []
    for k, (low, high) in enumerate(halos):
        dim = lead + k
        size = block.shape[dim]
        out.append(jnp.concatenate([lax.slice_in_dim(block, 1, size, axis=dim), high], axis=dim))
        out.append(jnp.concatenate([low, lax.slice_in_dim(block, 0, size - 1, axis=dim)], axis=dim))
    last = block.ndim - 1
    size = block.shape[last]
    zero = jnp.zeros_like(lax.slice_in_dim(block, 0, 1, axis=last))
    out.append(jnp.concatenate([lax.slice_in_dim(block, 1, size, axis=last), zero], axis=last))
    out.append(jnp.concatenate([zero, lax.slice_in_dim(block, 0, size - 1, axis=last)], axis=last))
    return out


def bernoulli(value):
    small = jnp.abs(value) < 0.0001
    safe = jnp.where(small, jnp.float32(1.0), value)
    return jnp.where(small, 1.0 - 0.5 * value, safe / jnp.expm1(safe))


def per_device(
    electrostatic_voltages,
    initial_electrons,
    creation_amounts,
    annihilation_coefficient,
    crystal_orientation_class,
    crystal_barrier_shift,
    restrict_matrix_first,
    restrict_matrix_second,
    restrict_matrix_third,
    cooling_coefficient,
    initial_warming,
):
    upper_limit = lax.Precision.HIGHEST
    slab_cells = electrostatic_voltages.shape[0]
    slabs = lax.axis_size("slab")
    me = lax.axis_index("slab")
    effective = electrostatic_voltages
    for grain in range(GRAINS):
        effective = effective + jnp.where(
            crystal_orientation_class == grain, crystal_barrier_shift[grain], jnp.float32(0.0)
        )
    device_sides = (("slab", 0), ("gy", 1))
    both = jnp.stack([effective, initial_electrons])
    both_halos = face_halos(both, (("slab", 1), ("gy", 2)))
    beside_both = neighbours_of(both, both_halos, lead=1)
    beside_all = [b[0] for b in beside_both]
    voltage_gradients = [leftover_portion - effective for leftover_portion in beside_all]
    bernoulli_coefficients = [bernoulli(voltage_gradient) for voltage_gradient in voltage_gradients]
    denominator_quantity = annihilation_coefficient
    for bernoulli_coefficient, voltage_gradient in zip(bernoulli_coefficients, voltage_gradients):
        denominator_quantity = denominator_quantity + (bernoulli_coefficient + voltage_gradient)

    def sweep(beside):
        fraction_top_quantity = creation_amounts
        for bernoulli_coefficient, leftover_portion in zip(bernoulli_coefficients, beside):
            fraction_top_quantity = fraction_top_quantity + bernoulli_coefficient * leftover_portion
        return fraction_top_quantity / denominator_quantity

    electron_concentration = sweep([b[1] for b in beside_both])
    electron_concentration = sweep(
        neighbours_of(electron_concentration, face_halos(electron_concentration, device_sides))
    )
    n_final = electron_concentration
    y_low, y_high = face_halos(n_final, (("gy", 1),))[0]
    zero_x = jnp.zeros_like(n_final[:1])
    beside_final = neighbours_of(n_final, [(zero_x, zero_x), (y_low, y_high)])
    joule_power_input = jnp.zeros_like(n_final)
    for bernoulli_coefficient, voltage_gradient, leftover_portion in zip(
        bernoulli_coefficients, voltage_gradients, beside_final
    ):
        joule_power_input = joule_power_input + voltage_gradient * (
            bernoulli_coefficient * leftover_portion
            - (bernoulli_coefficient + voltage_gradient) * n_final
        )
    joule_power_input = 0.5 * joule_power_input
    up_x, down_x = voltage_gradients[0], voltage_gradients[1]
    bup_x, bdown_x = bernoulli_coefficients[0], bernoulli_coefficients[1]
    heat_left = -0.5 * (down_x[:1] * ((bdown_x[:1] + down_x[:1]) * n_final[:1]))
    heat_right = -0.5 * (up_x[-1:] * ((bup_x[-1:] + up_x[-1:]) * n_final[-1:]))
    heat_ext = jnp.concatenate([heat_left, joule_power_input, heat_right], axis=0)

    padded_first = jnp.pad(restrict_matrix_first, ((1, 1), (1, 1)))
    ratio = slab_cells // 2
    columns_ext = lax.dynamic_slice(
        padded_first, (me * ratio, me * slab_cells), (BAND, slab_cells + 2)
    )
    columns = columns_ext[:, 1 : 1 + slab_cells]
    along_y = jnp.einsum(
        "ty,xyz->xtz", restrict_matrix_second, heat_ext, precision=upper_limit
    )
    along_z = jnp.einsum("cz,xtz->ctx", restrict_matrix_third, along_y, precision=upper_limit)
    piece = jnp.einsum("ctx,ax->cta", along_z, columns_ext, precision=upper_limit)
    chunk_c = piece.shape[0] // slabs
    piece = piece.reshape(slabs, chunk_c, piece.shape[1], BAND)
    got = lax.all_to_all(piece, "slab", 0, 0, tiled=False)
    main = got[..., 1 : 1 + ratio]
    zero_row = jnp.zeros_like(got[:1, ..., 0])
    left = jnp.concatenate([got[1:, ..., 0], zero_row], axis=0)
    right = jnp.concatenate([zero_row, got[:-1, ..., ratio + 1]], axis=0)
    main = main.at[..., ratio - 1].add(left)
    main = main.at[..., 0].add(right)
    source = jnp.transpose(main, (1, 2, 0, 3)).reshape(chunk_c, main.shape[2], slabs * ratio)

    stacked = jnp.stack([initial_warming, source, 6.0 + cooling_coefficient])
    depths = (HEAT_SWEEPS, 8)
    for (axis, dim), depth in zip((("slab", 1), ("gy", 2)), depths):
        count = lax.axis_size(axis)
        forward = [(i, i + 1) for i in range(count - 1)]
        backward = [(i + 1, i) for i in range(count - 1)]
        size = stacked.shape[dim]
        low = lax.ppermute(lax.slice_in_dim(stacked, size - depth, size, axis=dim), axis, forward)
        high = lax.ppermute(lax.slice_in_dim(stacked, 0, depth, axis=dim), axis, backward)
        stacked = jnp.concatenate([low, stacked, high], axis=dim)
    tc, tb = initial_warming.shape[0], initial_warming.shape[1]
    c_index = lax.broadcasted_iota(jnp.int32, stacked.shape[1:], 0) + (me * tc - depths[0])
    b_index = lax.broadcasted_iota(jnp.int32, stacked.shape[1:], 1) + (
        lax.axis_index("gy") * tb - depths[1]
    )
    inside = (
        (c_index >= 0)
        & (c_index < slabs * tc)
        & (b_index >= 0)
        & (b_index < lax.axis_size("gy") * tb)
    )
    warm = stacked[0]
    source_ext, scale_ext = stacked[1], stacked[2]
    for repeat in range(HEAT_SWEEPS):
        padded = jnp.pad(warm, 1)
        total = source_ext
        for leftover_portion in (
            padded[2:, 1:-1, 1:-1],
            padded[:-2, 1:-1, 1:-1],
            padded[1:-1, 2:, 1:-1],
            padded[1:-1, :-2, 1:-1],
            padded[1:-1, 1:-1, 2:],
            padded[1:-1, 1:-1, :-2],
        ):
            total = total + leftover_portion
        warm = jnp.where(inside, total / scale_ext, 0.0)
    warming_distribution = warm[depths[0] : depths[0] + tc, depths[1] : depths[1] + tb]

    padded_warm = jnp.pad(warming_distribution, ((0, 0), (0, 0), (1, 1)))
    windows = jnp.stack(
        [padded_warm[..., ratio * s : ratio * s + BAND] for s in range(slabs)]
    )
    got_warm = lax.all_to_all(windows, "slab", 0, 0, tiled=False)
    got_warm = got_warm.reshape(slabs * chunk_c, got_warm.shape[2], BAND)
    spread = jnp.einsum("cta,ax->ctx", got_warm, columns, precision=upper_limit)
    raised_field = jnp.einsum(
        "ctx,cz->xtz", spread, restrict_matrix_third, precision=upper_limit
    )
    fine_mesh_warming = 16.0 * jnp.einsum(
        "hc,qhk->qck", restrict_matrix_second, raised_field, precision=upper_limit
    )
    return (electron_concentration, warming_distribution, fine_mesh_warming)


def solution(mesh):
    in_specs = (
        P("slab", "gy", None),
        P("slab", "gy", None),
        P("slab", "gy", None),
        P("slab", "gy", None),
        P("slab", "gy", None),
        P(),
        P(),
        P("gy", None),
        P(),
        P("slab", "gy", None),
        P("slab", "gy", None),
    )
    out_specs = (P("slab", "gy", None), P("slab", "gy", None), P("slab", "gy", None))
    return jax.shard_map(
        per_device, mesh=mesh, in_specs=in_specs, out_specs=out_specs, check_vma=False
    )
```

```python
import jax
import jax.numpy as jnp
from jax import lax
from jax.sharding import PartitionSpec as P

GRAINS = 4
HEAT_SWEEPS = 3
BAND = 6


def face_halos(block, sides):
    halos = []
    for axis, dim in sides:
        count = lax.axis_size(axis)
        forward = [(i, i + 1) for i in range(count - 1)]
        backward = [(i + 1, i) for i in range(count - 1)]
        size = block.shape[dim]
        low = lax.ppermute(lax.slice_in_dim(block, size - 1, size, axis=dim), axis, forward)
        high = lax.ppermute(lax.slice_in_dim(block, 0, 1, axis=dim), axis, backward)
        halos.append((low, high))
    return halos


def neighbours_of(block, halos, lead=0):
    out = []
    for k, (low, high) in enumerate(halos):
        dim = lead + k
        size = block.shape[dim]
        out.append(jnp.concatenate([lax.slice_in_dim(block, 1, size, axis=dim), high], axis=dim))
        out.append(jnp.concatenate([low, lax.slice_in_dim(block, 0, size - 1, axis=dim)], axis=dim))
    last = block.ndim - 1
    size = block.shape[last]
    zero = jnp.zeros_like(lax.slice_in_dim(block, 0, 1, axis=last))
    out.append(jnp.concatenate([lax.slice_in_dim(block, 1, size, axis=last), zero], axis=last))
    out.append(jnp.concatenate([zero, lax.slice_in_dim(block, 0, size - 1, axis=last)], axis=last))
    return out


def bernoulli(value):
    small = jnp.abs(value) < 0.0001
    safe = jnp.where(small, jnp.float32(1.0), value)
    return jnp.where(small, 1.0 - 0.5 * value, safe / jnp.expm1(safe))


def per_device(
    electrostatic_voltages,
    initial_electrons,
    creation_amounts,
    annihilation_coefficient,
    crystal_orientation_class,
    crystal_barrier_shift,
    restrict_matrix_first,
    restrict_matrix_second,
    restrict_matrix_third,
    cooling_coefficient,
    initial_warming,
):
    upper_limit = lax.Precision.HIGHEST
    slab_cells = electrostatic_voltages.shape[0]
    slabs = lax.axis_size("slab")
    me = lax.axis_index("slab")
    effective = electrostatic_voltages
    for grain in range(GRAINS):
        effective = effective + jnp.where(
            crystal_orientation_class == grain, crystal_barrier_shift[grain], jnp.float32(0.0)
        )
    device_sides = (("slab", 0), ("gy", 1))
    both = jnp.stack([effective, initial_electrons])
    both_halos = face_halos(both, (("slab", 1), ("gy", 2)))
    beside_both = neighbours_of(both, both_halos, lead=1)
    beside_all = [b[0] for b in beside_both]
    voltage_gradients = [leftover_portion - effective for leftover_portion in beside_all]
    bernoulli_coefficients = [bernoulli(voltage_gradient) for voltage_gradient in voltage_gradients]
    denominator_quantity = annihilation_coefficient
    for bernoulli_coefficient, voltage_gradient in zip(bernoulli_coefficients, voltage_gradients):
        denominator_quantity = denominator_quantity + (bernoulli_coefficient + voltage_gradient)

    def sweep(beside):
        fraction_top_quantity = creation_amounts
        for bernoulli_coefficient, leftover_portion in zip(bernoulli_coefficients, beside):
            fraction_top_quantity = fraction_top_quantity + bernoulli_coefficient * leftover_portion
        return fraction_top_quantity / denominator_quantity

    electron_concentration = sweep([b[1] for b in beside_both])
    electron_concentration = sweep(
        neighbours_of(electron_concentration, face_halos(electron_concentration, device_sides))
    )
    n_final = electron_concentration
    y_low, y_high = face_halos(n_final, (("gy", 1),))[0]
    zero_x = jnp.zeros_like(n_final[:1])
    beside_final = neighbours_of(n_final, [(zero_x, zero_x), (y_low, y_high)])
    joule_power_input = jnp.zeros_like(n_final)
    for bernoulli_coefficient, voltage_gradient, leftover_portion in zip(
        bernoulli_coefficients, voltage_gradients, beside_final
    ):
        joule_power_input = joule_power_input + voltage_gradient * (
            bernoulli_coefficient * leftover_portion
            - (bernoulli_coefficient + voltage_gradient) * n_final
        )
    joule_power_input = 0.5 * joule_power_input
    up_x, down_x = voltage_gradients[0], voltage_gradients[1]
    bup_x, bdown_x = bernoulli_coefficients[0], bernoulli_coefficients[1]
    heat_left = -0.5 * (down_x[:1] * ((bdown_x[:1] + down_x[:1]) * n_final[:1]))
    heat_right = -0.5 * (up_x[-1:] * ((bup_x[-1:] + up_x[-1:]) * n_final[-1:]))
    heat_ext = jnp.concatenate([heat_left, joule_power_input, heat_right], axis=0)

    padded_first = jnp.pad(restrict_matrix_first, ((1, 1), (1, 1)))
    ratio = slab_cells // 2
    columns_ext = lax.dynamic_slice(
        padded_first, (me * ratio, me * slab_cells), (BAND, slab_cells + 2)
    )
    columns = columns_ext[:, 1 : 1 + slab_cells]
    along_y = jnp.einsum(
        "ty,xyz->xtz", restrict_matrix_second, heat_ext, precision=upper_limit
    )
    along_z = jnp.einsum("cz,xtz->ctx", restrict_matrix_third, along_y, precision=upper_limit)
    piece = jnp.einsum("ctx,ax->cta", along_z, columns_ext, precision=upper_limit)
    chunk_c = piece.shape[0] // slabs
    piece = piece.reshape(slabs, chunk_c, piece.shape[1], BAND)
    got = lax.all_to_all(piece, "slab", 0, 0, tiled=False)
    main = got[..., 1 : 1 + ratio]
    zero_row = jnp.zeros_like(got[:1, ..., 0])
    left = jnp.concatenate([got[1:, ..., 0], zero_row], axis=0)
    right = jnp.concatenate([zero_row, got[:-1, ..., ratio + 1]], axis=0)
    main = main.at[..., ratio - 1].add(left)
    main = main.at[..., 0].add(right)
    source = jnp.transpose(main, (1, 2, 0, 3)).reshape(chunk_c, main.shape[2], slabs * ratio)

    stacked = jnp.stack([initial_warming, source, 6.0 + cooling_coefficient])
    depths = (HEAT_SWEEPS, 8)
    for (axis, dim), depth in zip((("slab", 1), ("gy", 2)), depths):
        count = lax.axis_size(axis)
        forward = [(i, i + 1) for i in range(count - 1)]
        backward = [(i + 1, i) for i in range(count - 1)]
        size = stacked.shape[dim]
        low = lax.ppermute(lax.slice_in_dim(stacked, size - depth, size, axis=dim), axis, forward)
        high = lax.ppermute(lax.slice_in_dim(stacked, 0, depth, axis=dim), axis, backward)
        stacked = jnp.concatenate([low, stacked, high], axis=dim)
    tc, tb = initial_warming.shape[0], initial_warming.shape[1]
    c_index = lax.broadcasted_iota(jnp.int32, stacked.shape[1:], 0) + (me * tc - depths[0])
    b_index = lax.broadcasted_iota(jnp.int32, stacked.shape[1:], 1) + (
        lax.axis_index("gy") * tb - depths[1]
    )
    inside = (
        (c_index >= 0)
        & (c_index < slabs * tc)
        & (b_index >= 0)
        & (b_index < lax.axis_size("gy") * tb)
    )
    warm = stacked[0]
    source_ext, scale_ext = stacked[1], stacked[2]
    for repeat in range(HEAT_SWEEPS):
        padded = jnp.pad(warm, 1)
        total = source_ext
        for leftover_portion in (
            padded[2:, 1:-1, 1:-1],
            padded[:-2, 1:-1, 1:-1],
            padded[1:-1, 2:, 1:-1],
            padded[1:-1, :-2, 1:-1],
            padded[1:-1, 1:-1, 2:],
            padded[1:-1, 1:-1, :-2],
        ):
            total = total + leftover_portion
        warm = jnp.where(inside, total / scale_ext, 0.0)
    warming_distribution = warm[depths[0] : depths[0] + tc, depths[1] : depths[1] + tb]

    a_count = warming_distribution.shape[2]
    pick = (
        lax.broadcasted_iota(jnp.int32, (slabs, BAND, a_count), 2)
        == lax.broadcasted_iota(jnp.int32, (slabs, BAND, a_count), 0) * ratio
        + lax.broadcasted_iota(jnp.int32, (slabs, BAND, a_count), 1)
        - 1
    ).astype(jnp.float32)
    windows = jnp.einsum("ska,cba->skcb", pick, warming_distribution, precision=upper_limit)
    got_warm = lax.all_to_all(windows, "slab", 0, 0, tiled=False)
    spread = jnp.einsum("skcb,kx->scbx", got_warm, columns, precision=upper_limit)
    third = restrict_matrix_third.reshape(slabs, chunk_c, restrict_matrix_third.shape[1])
    raised_field = jnp.einsum("scbx,scz->xbz", spread, third, precision=upper_limit)
    fine_mesh_warming = 16.0 * jnp.einsum(
        "hc,qhk->qck", restrict_matrix_second, raised_field, precision=upper_limit
    )
    return (electron_concentration, warming_distribution, fine_mesh_warming)


def solution(mesh):
    in_specs = (
        P("slab", "gy", None),
        P("slab", "gy", None),
        P("slab", "gy", None),
        P("slab", "gy", None),
        P("slab", "gy", None),
        P(),
        P(),
        P("gy", None),
        P(),
        P("slab", "gy", None),
        P("slab", "gy", None),
    )
    out_specs = (P("slab", "gy", None), P("slab", "gy", None), P("slab", "gy", None))
    return jax.shard_map(
        per_device, mesh=mesh, in_specs=in_specs, out_specs=out_specs, check_vma=False
    )
```

```python
import jax
import jax.numpy as jnp
from jax import lax
from jax.sharding import PartitionSpec as P

GRAINS = 4
HEAT_SWEEPS = 3
BAND = 6


def face_halos(block, sides):
    halos = []
    for axis, dim in sides:
        count = lax.axis_size(axis)
        forward = [(i, i + 1) for i in range(count - 1)]
        backward = [(i + 1, i) for i in range(count - 1)]
        size = block.shape[dim]
        low = lax.ppermute(lax.slice_in_dim(block, size - 1, size, axis=dim), axis, forward)
        high = lax.ppermute(lax.slice_in_dim(block, 0, 1, axis=dim), axis, backward)
        halos.append((low, high))
    return halos


def neighbours_of(block, halos, lead=0):
    out = []
    for k, (low, high) in enumerate(halos):
        dim = lead + k
        size = block.shape[dim]
        out.append(jnp.concatenate([lax.slice_in_dim(block, 1, size, axis=dim), high], axis=dim))
        out.append(jnp.concatenate([low, lax.slice_in_dim(block, 0, size - 1, axis=dim)], axis=dim))
    last = block.ndim - 1
    size = block.shape[last]
    zero = jnp.zeros_like(lax.slice_in_dim(block, 0, 1, axis=last))
    out.append(jnp.concatenate([lax.slice_in_dim(block, 1, size, axis=last), zero], axis=last))
    out.append(jnp.concatenate([zero, lax.slice_in_dim(block, 0, size - 1, axis=last)], axis=last))
    return out


def bernoulli(value):
    small = jnp.abs(value) < 0.0001
    safe = jnp.where(small, jnp.float32(1.0), value)
    return jnp.where(small, 1.0 - 0.5 * value, safe / jnp.expm1(safe))


def per_device(
    electrostatic_voltages,
    initial_electrons,
    creation_amounts,
    annihilation_coefficient,
    crystal_orientation_class,
    crystal_barrier_shift,
    restrict_matrix_first,
    restrict_matrix_second,
    restrict_matrix_third,
    cooling_coefficient,
    initial_warming,
):
    upper_limit = lax.Precision.HIGHEST
    slab_cells = electrostatic_voltages.shape[0]
    slabs = lax.axis_size("slab")
    me = lax.axis_index("slab")
    def effective_of(voltages, classes):
        value = voltages
        for grain in range(GRAINS):
            value = value + jnp.where(
                classes == grain, crystal_barrier_shift[grain], jnp.float32(0.0)
            )
        return value

    effective = effective_of(electrostatic_voltages, crystal_orientation_class)
    device_sides = (("slab", 0), ("gy", 1))
    halos_in = []
    for axis, dim in device_sides:
        count = lax.axis_size(axis)
        forward = [(i, i + 1) for i in range(count - 1)]
        backward = [(i + 1, i) for i in range(count - 1)]
        size = effective.shape[dim]
        layers = []
        for where in (size - 1, 0):
            pick = lambda a: lax.slice_in_dim(a, where, where + 1, axis=dim)
            layers.append(
                jnp.stack(
                    [
                        effective_of(pick(electrostatic_voltages), pick(crystal_orientation_class)),
                        pick(initial_electrons),
                    ]
                )
            )
        low = lax.ppermute(layers[0], axis, forward)
        high = lax.ppermute(layers[1], axis, backward)
        halos_in.append((low, high))
    eff_halos = [(low[0], high[0]) for low, high in halos_in]
    start_halos = [(low[1], high[1]) for low, high in halos_in]

    def around(block, halos, lo, hi):
        (x_low, x_high), (y_low, y_high) = halos
        count = block.shape[0]
        centre = block[lo:hi]
        if hi < count:
            up = block[lo + 1 : hi + 1]
        else:
            up = jnp.concatenate([block[lo + 1 :], x_high], axis=0)
        if lo > 0:
            down = block[lo - 1 : hi - 1]
        else:
            down = jnp.concatenate([x_low, block[: hi - 1]], axis=0)
        zero = jnp.zeros_like(centre[..., :1])
        return [
            up,
            down,
            jnp.concatenate([centre[:, 1:], y_high[lo:hi]], axis=1),
            jnp.concatenate([y_low[lo:hi], centre[:, :-1]], axis=1),
            jnp.concatenate([centre[..., 1:], zero], axis=2),
            jnp.concatenate([zero, centre[..., :-1]], axis=2),
        ]

    def coefficients(lo, hi):
        centre = effective[lo:hi]
        gradients = [b - centre for b in around(effective, eff_halos, lo, hi)]
        coeffs = [bernoulli(g) for g in gradients]
        denominator = annihilation_coefficient[lo:hi]
        for bc, vg in zip(coeffs, gradients):
            denominator = denominator + (bc + vg)
        return gradients, coeffs, denominator

    def sweep_part(density, halos, lo, hi):
        _, coeffs, denominator = coefficients(lo, hi)
        top = creation_amounts[lo:hi]
        for bc, nb in zip(coeffs, around(density, halos, lo, hi)):
            top = top + bc * nb
        return top / denominator

    def sweep(density, halos):
        count = density.shape[0]
        inner = lax.optimization_barrier(sweep_part(density, halos, 1, count - 1))
        first = sweep_part(density, halos, 0, 1)
        last = sweep_part(density, halos, count - 1, count)
        return jnp.concatenate([first, inner, last], axis=0)

    electron_concentration = sweep(initial_electrons, start_halos)
    electron_concentration = sweep(
        electron_concentration, face_halos(electron_concentration, device_sides)
    )
    voltage_gradients, bernoulli_coefficients, _ = coefficients(0, effective.shape[0])
    n_final = electron_concentration
    y_low, y_high = face_halos(n_final, (("gy", 1),))[0]
    zero_x = jnp.zeros_like(n_final[:1])
    beside_final = neighbours_of(n_final, [(zero_x, zero_x), (y_low, y_high)])
    joule_power_input = jnp.zeros_like(n_final)
    for bernoulli_coefficient, voltage_gradient, leftover_portion in zip(
        bernoulli_coefficients, voltage_gradients, beside_final
    ):
        joule_power_input = joule_power_input + voltage_gradient * (
            bernoulli_coefficient * leftover_portion
            - (bernoulli_coefficient + voltage_gradient) * n_final
        )
    joule_power_input = 0.5 * joule_power_input
    up_x, down_x = voltage_gradients[0], voltage_gradients[1]
    bup_x, bdown_x = bernoulli_coefficients[0], bernoulli_coefficients[1]
    heat_left = -0.5 * (down_x[:1] * ((bdown_x[:1] + down_x[:1]) * n_final[:1]))
    heat_right = -0.5 * (up_x[-1:] * ((bup_x[-1:] + up_x[-1:]) * n_final[-1:]))
    heat_ext = jnp.concatenate([heat_left, joule_power_input, heat_right], axis=0)

    padded_first = jnp.pad(restrict_matrix_first, ((1, 1), (1, 1)))
    ratio = slab_cells // 2
    columns_ext = lax.dynamic_slice(
        padded_first, (me * ratio, me * slab_cells), (BAND, slab_cells + 2)
    )
    columns = columns_ext[:, 1 : 1 + slab_cells]
    along_y = jnp.einsum(
        "ty,xyz->xtz", restrict_matrix_second, heat_ext, precision=upper_limit
    )
    along_z = jnp.einsum("cz,xtz->ctx", restrict_matrix_third, along_y, precision=upper_limit)
    piece = jnp.einsum("ctx,ax->cta", along_z, columns_ext, precision=upper_limit)
    chunk_c = piece.shape[0] // slabs
    piece = piece.reshape(slabs, chunk_c, piece.shape[1], BAND)
    got = lax.all_to_all(piece, "slab", 0, 0, tiled=False)
    main = got[..., 1 : 1 + ratio]
    zero_row = jnp.zeros_like(got[:1, ..., 0])
    left = jnp.concatenate([got[1:, ..., 0], zero_row], axis=0)
    right = jnp.concatenate([zero_row, got[:-1, ..., ratio + 1]], axis=0)
    main = main.at[..., ratio - 1].add(left)
    main = main.at[..., 0].add(right)
    source = jnp.transpose(main, (1, 2, 0, 3)).reshape(chunk_c, main.shape[2], slabs * ratio)

    stacked = jnp.stack([initial_warming, source, 6.0 + cooling_coefficient])
    depths = (HEAT_SWEEPS, 8)
    for (axis, dim), depth in zip((("slab", 1), ("gy", 2)), depths):
        count = lax.axis_size(axis)
        forward = [(i, i + 1) for i in range(count - 1)]
        backward = [(i + 1, i) for i in range(count - 1)]
        size = stacked.shape[dim]
        low = lax.ppermute(lax.slice_in_dim(stacked, size - depth, size, axis=dim), axis, forward)
        high = lax.ppermute(lax.slice_in_dim(stacked, 0, depth, axis=dim), axis, backward)
        stacked = jnp.concatenate([low, stacked, high], axis=dim)
    tc, tb = initial_warming.shape[0], initial_warming.shape[1]
    c_index = lax.broadcasted_iota(jnp.int32, stacked.shape[1:], 0) + (me * tc - depths[0])
    b_index = lax.broadcasted_iota(jnp.int32, stacked.shape[1:], 1) + (
        lax.axis_index("gy") * tb - depths[1]
    )
    inside = (
        (c_index >= 0)
        & (c_index < slabs * tc)
        & (b_index >= 0)
        & (b_index < lax.axis_size("gy") * tb)
    )
    warm = stacked[0]
    source_ext, scale_ext = stacked[1], stacked[2]
    for repeat in range(HEAT_SWEEPS):
        padded = jnp.pad(warm, 1)
        total = source_ext
        for leftover_portion in (
            padded[2:, 1:-1, 1:-1],
            padded[:-2, 1:-1, 1:-1],
            padded[1:-1, 2:, 1:-1],
            padded[1:-1, :-2, 1:-1],
            padded[1:-1, 1:-1, 2:],
            padded[1:-1, 1:-1, :-2],
        ):
            total = total + leftover_portion
        warm = jnp.where(inside, total / scale_ext, 0.0)
    warming_distribution = warm[depths[0] : depths[0] + tc, depths[1] : depths[1] + tb]

    a_count = warming_distribution.shape[2]
    pick = (
        lax.broadcasted_iota(jnp.int32, (slabs, BAND, a_count), 2)
        == lax.broadcasted_iota(jnp.int32, (slabs, BAND, a_count), 0) * ratio
        + lax.broadcasted_iota(jnp.int32, (slabs, BAND, a_count), 1)
        - 1
    ).astype(jnp.float32)
    windows = jnp.einsum("ska,cba->skcb", pick, warming_distribution, precision=upper_limit)
    got_warm = lax.all_to_all(windows, "slab", 0, 0, tiled=False)
    spread = jnp.einsum("skcb,kx->scbx", got_warm, columns, precision=upper_limit)
    third = restrict_matrix_third.reshape(slabs, chunk_c, restrict_matrix_third.shape[1])
    raised_field = jnp.einsum("scbx,scz->xbz", spread, third, precision=upper_limit)
    fine_mesh_warming = 16.0 * jnp.einsum(
        "hc,qhk->qck", restrict_matrix_second, raised_field, precision=upper_limit
    )
    return (electron_concentration, warming_distribution, fine_mesh_warming)


def solution(mesh):
    in_specs = (
        P("slab", "gy", None),
        P("slab", "gy", None),
        P("slab", "gy", None),
        P("slab", "gy", None),
        P("slab", "gy", None),
        P(),
        P(),
        P("gy", None),
        P(),
        P("slab", "gy", None),
        P("slab", "gy", None),
    )
    out_specs = (P("slab", "gy", None), P("slab", "gy", None), P("slab", "gy", None))
    return jax.shard_map(
        per_device, mesh=mesh, in_specs=in_specs, out_specs=out_specs, check_vma=False
    )
```

```python
import jax
import jax.numpy as jnp
from jax import lax
from jax.sharding import PartitionSpec as P

GRAINS = 4
HEAT_SWEEPS = 3
BAND = 6


def face_halos(block, sides):
    halos = []
    for axis, dim in sides:
        count = lax.axis_size(axis)
        forward = [(i, i + 1) for i in range(count - 1)]
        backward = [(i + 1, i) for i in range(count - 1)]
        size = block.shape[dim]
        low = lax.ppermute(lax.slice_in_dim(block, size - 1, size, axis=dim), axis, forward)
        high = lax.ppermute(lax.slice_in_dim(block, 0, 1, axis=dim), axis, backward)
        halos.append((low, high))
    return halos


def face_halos_of(blocks, sides):
    halos = [[] for _ in blocks]
    for axis, dim in sides:
        count = lax.axis_size(axis)
        forward = [(i, i + 1) for i in range(count - 1)]
        backward = [(i + 1, i) for i in range(count - 1)]
        size = blocks[0].shape[dim]
        low = lax.ppermute(
            jnp.stack([lax.slice_in_dim(b, size - 1, size, axis=dim) for b in blocks]),
            axis,
            forward,
        )
        high = lax.ppermute(
            jnp.stack([lax.slice_in_dim(b, 0, 1, axis=dim) for b in blocks]), axis, backward
        )
        for k in range(len(blocks)):
            halos[k].append((low[k], high[k]))
    return halos


def neighbours_of(block, halos, lead=0):
    out = []
    for k, (low, high) in enumerate(halos):
        dim = lead + k
        size = block.shape[dim]
        out.append(jnp.concatenate([lax.slice_in_dim(block, 1, size, axis=dim), high], axis=dim))
        out.append(jnp.concatenate([low, lax.slice_in_dim(block, 0, size - 1, axis=dim)], axis=dim))
    last = block.ndim - 1
    size = block.shape[last]
    zero = jnp.zeros_like(lax.slice_in_dim(block, 0, 1, axis=last))
    out.append(jnp.concatenate([lax.slice_in_dim(block, 1, size, axis=last), zero], axis=last))
    out.append(jnp.concatenate([zero, lax.slice_in_dim(block, 0, size - 1, axis=last)], axis=last))
    return out


def bernoulli(value):
    small = jnp.abs(value) < 0.0001
    safe = jnp.where(small, jnp.float32(1.0), value)
    return jnp.where(small, 1.0 - 0.5 * value, safe / jnp.expm1(safe))


def per_device(
    electrostatic_voltages,
    initial_electrons,
    creation_amounts,
    annihilation_coefficient,
    crystal_orientation_class,
    crystal_barrier_shift,
    restrict_matrix_first,
    restrict_matrix_second,
    restrict_matrix_third,
    cooling_coefficient,
    initial_warming,
):
    upper_limit = lax.Precision.HIGHEST
    slab_cells = electrostatic_voltages.shape[0]
    slabs = lax.axis_size("slab")
    me = lax.axis_index("slab")
    effective = electrostatic_voltages
    for grain in range(GRAINS):
        effective = effective + jnp.where(
            crystal_orientation_class == grain, crystal_barrier_shift[grain], jnp.float32(0.0)
        )
    device_sides = (("slab", 0), ("gy", 1))
    eff_halos, start_halos = face_halos_of([effective, initial_electrons], device_sides)
    beside_all = neighbours_of(effective, eff_halos)
    voltage_gradients = [leftover_portion - effective for leftover_portion in beside_all]
    bernoulli_coefficients = list(
        lax.optimization_barrier(tuple(bernoulli(vg) for vg in voltage_gradients[:4]))
    ) + [bernoulli(vg) for vg in voltage_gradients[4:]]
    denominator_quantity = annihilation_coefficient
    for bernoulli_coefficient, voltage_gradient in zip(bernoulli_coefficients, voltage_gradients):
        denominator_quantity = denominator_quantity + (bernoulli_coefficient + voltage_gradient)

    def sweep(beside):
        fraction_top_quantity = creation_amounts
        for bernoulli_coefficient, leftover_portion in zip(bernoulli_coefficients, beside):
            fraction_top_quantity = fraction_top_quantity + bernoulli_coefficient * leftover_portion
        return fraction_top_quantity / denominator_quantity

    electron_concentration = sweep(neighbours_of(initial_electrons, start_halos))
    electron_concentration = sweep(
        neighbours_of(electron_concentration, face_halos(electron_concentration, device_sides))
    )
    n_final = electron_concentration
    y_low, y_high = face_halos(n_final, (("gy", 1),))[0]
    zero_x = jnp.zeros_like(n_final[:1])
    beside_final = neighbours_of(n_final, [(zero_x, zero_x), (y_low, y_high)])
    joule_power_input = jnp.zeros_like(n_final)
    for bernoulli_coefficient, voltage_gradient, leftover_portion in zip(
        bernoulli_coefficients, voltage_gradients, beside_final
    ):
        joule_power_input = joule_power_input + voltage_gradient * (
            bernoulli_coefficient * leftover_portion
            - (bernoulli_coefficient + voltage_gradient) * n_final
        )
    joule_power_input = 0.5 * joule_power_input
    up_x, down_x = voltage_gradients[0], voltage_gradients[1]
    bup_x, bdown_x = bernoulli_coefficients[0], bernoulli_coefficients[1]
    heat_left = -0.5 * (down_x[:1] * ((bdown_x[:1] + down_x[:1]) * n_final[:1]))
    heat_right = -0.5 * (up_x[-1:] * ((bup_x[-1:] + up_x[-1:]) * n_final[-1:]))
    heat_ext = jnp.concatenate([heat_left, joule_power_input, heat_right], axis=0)

    padded_first = jnp.pad(restrict_matrix_first, ((1, 1), (1, 1)))
    ratio = slab_cells // 2
    columns_ext = lax.dynamic_slice(
        padded_first, (me * ratio, me * slab_cells), (BAND, slab_cells + 2)
    )
    columns = columns_ext[:, 1 : 1 + slab_cells]
    along_y = jnp.einsum(
        "ty,xyz->xtz", restrict_matrix_second, heat_ext, precision=upper_limit
    )
    along_z = jnp.einsum("cz,xtz->ctx", restrict_matrix_third, along_y, precision=upper_limit)
    piece = jnp.einsum("ctx,ax->cta", along_z, columns_ext, precision=upper_limit)
    chunk_c = piece.shape[0] // slabs
    piece = piece.reshape(slabs, chunk_c, piece.shape[1], BAND)
    got = lax.all_to_all(piece, "slab", 0, 0, tiled=False)
    main = got[..., 1 : 1 + ratio]
    zero_row = jnp.zeros_like(got[:1, ..., 0])
    left = jnp.concatenate([got[1:, ..., 0], zero_row], axis=0)
    right = jnp.concatenate([zero_row, got[:-1, ..., ratio + 1]], axis=0)
    main = main.at[..., ratio - 1].add(left)
    main = main.at[..., 0].add(right)
    source = jnp.transpose(main, (1, 2, 0, 3)).reshape(chunk_c, main.shape[2], slabs * ratio)

    stacked = jnp.stack([initial_warming, source, 6.0 + cooling_coefficient])
    depths = (HEAT_SWEEPS, 8)
    for (axis, dim), depth in zip((("slab", 1), ("gy", 2)), depths):
        count = lax.axis_size(axis)
        forward = [(i, i + 1) for i in range(count - 1)]
        backward = [(i + 1, i) for i in range(count - 1)]
        size = stacked.shape[dim]
        low = lax.ppermute(lax.slice_in_dim(stacked, size - depth, size, axis=dim), axis, forward)
        high = lax.ppermute(lax.slice_in_dim(stacked, 0, depth, axis=dim), axis, backward)
        stacked = jnp.concatenate([low, stacked, high], axis=dim)
    tc, tb = initial_warming.shape[0], initial_warming.shape[1]
    c_index = lax.broadcasted_iota(jnp.int32, stacked.shape[1:], 0) + (me * tc - depths[0])
    b_index = lax.broadcasted_iota(jnp.int32, stacked.shape[1:], 1) + (
        lax.axis_index("gy") * tb - depths[1]
    )
    inside = (
        (c_index >= 0)
        & (c_index < slabs * tc)
        & (b_index >= 0)
        & (b_index < lax.axis_size("gy") * tb)
    )
    warm = stacked[0]
    source_ext, scale_ext = stacked[1], stacked[2]
    for repeat in range(HEAT_SWEEPS):
        padded = jnp.pad(warm, 1)
        total = source_ext
        for leftover_portion in (
            padded[2:, 1:-1, 1:-1],
            padded[:-2, 1:-1, 1:-1],
            padded[1:-1, 2:, 1:-1],
            padded[1:-1, :-2, 1:-1],
            padded[1:-1, 1:-1, 2:],
            padded[1:-1, 1:-1, :-2],
        ):
            total = total + leftover_portion
        warm = jnp.where(inside, total / scale_ext, 0.0)
    warming_distribution = warm[depths[0] : depths[0] + tc, depths[1] : depths[1] + tb]

    a_count = warming_distribution.shape[2]
    pick = (
        lax.broadcasted_iota(jnp.int32, (slabs, BAND, a_count), 2)
        == lax.broadcasted_iota(jnp.int32, (slabs, BAND, a_count), 0) * ratio
        + lax.broadcasted_iota(jnp.int32, (slabs, BAND, a_count), 1)
        - 1
    ).astype(jnp.float32)
    windows = jnp.einsum("ska,cba->skcb", pick, warming_distribution, precision=upper_limit)
    got_warm = lax.all_to_all(windows, "slab", 0, 0, tiled=False)
    spread = jnp.einsum("skcb,kx->scbx", got_warm, columns, precision=upper_limit)
    third = restrict_matrix_third.reshape(slabs, chunk_c, restrict_matrix_third.shape[1])
    raised_field = jnp.einsum("scbx,scz->xbz", spread, third, precision=upper_limit)
    fine_mesh_warming = 16.0 * jnp.einsum(
        "hc,qhk->qck", restrict_matrix_second, raised_field, precision=upper_limit
    )
    return (electron_concentration, warming_distribution, fine_mesh_warming)


def solution(mesh):
    in_specs = (
        P("slab", "gy", None),
        P("slab", "gy", None),
        P("slab", "gy", None),
        P("slab", "gy", None),
        P("slab", "gy", None),
        P(),
        P(),
        P("gy", None),
        P(),
        P("slab", "gy", None),
        P("slab", "gy", None),
    )
    out_specs = (P("slab", "gy", None), P("slab", "gy", None), P("slab", "gy", None))
    return jax.shard_map(
        per_device, mesh=mesh, in_specs=in_specs, out_specs=out_specs, check_vma=False
    )
```

```python
import jax
import jax.numpy as jnp
from jax import lax
from jax.sharding import PartitionSpec as P

GRAINS = 4
HEAT_SWEEPS = 3
BAND = 6


def face_halos(block, sides):
    halos = []
    for axis, dim in sides:
        count = lax.axis_size(axis)
        forward = [(i, i + 1) for i in range(count - 1)]
        backward = [(i + 1, i) for i in range(count - 1)]
        size = block.shape[dim]
        low = lax.ppermute(lax.slice_in_dim(block, size - 1, size, axis=dim), axis, forward)
        high = lax.ppermute(lax.slice_in_dim(block, 0, 1, axis=dim), axis, backward)
        halos.append((low, high))
    return halos


def neighbours_of(block, halos, lead=0):
    out = []
    for k, (low, high) in enumerate(halos):
        dim = lead + k
        size = block.shape[dim]
        out.append(jnp.concatenate([lax.slice_in_dim(block, 1, size, axis=dim), high], axis=dim))
        out.append(jnp.concatenate([low, lax.slice_in_dim(block, 0, size - 1, axis=dim)], axis=dim))
    last = block.ndim - 1
    size = block.shape[last]
    zero = jnp.zeros_like(lax.slice_in_dim(block, 0, 1, axis=last))
    out.append(jnp.concatenate([lax.slice_in_dim(block, 1, size, axis=last), zero], axis=last))
    out.append(jnp.concatenate([zero, lax.slice_in_dim(block, 0, size - 1, axis=last)], axis=last))
    return out


def bernoulli(value):
    small = jnp.abs(value) < 0.0001
    safe = jnp.where(small, jnp.float32(1.0), value)
    return jnp.where(small, 1.0 - 0.5 * value, safe / jnp.expm1(safe))


def per_device(
    electrostatic_voltages,
    initial_electrons,
    creation_amounts,
    annihilation_coefficient,
    crystal_orientation_class,
    crystal_barrier_shift,
    restrict_matrix_first,
    restrict_matrix_second,
    restrict_matrix_third,
    cooling_coefficient,
    initial_warming,
):
    upper_limit = lax.Precision.HIGHEST
    slab_cells = electrostatic_voltages.shape[0]
    slabs = lax.axis_size("slab")
    me = lax.axis_index("slab")
    effective = electrostatic_voltages
    for grain in range(GRAINS):
        effective = effective + jnp.where(
            crystal_orientation_class == grain, crystal_barrier_shift[grain], jnp.float32(0.0)
        )
    device_sides = (("slab", 0), ("gy", 1))
    both = jnp.stack([effective, initial_electrons])
    both_halos = face_halos(both, (("slab", 1), ("gy", 2)))
    beside_both = neighbours_of(both, both_halos, lead=1)
    beside_all = [b[0] for b in beside_both]
    voltage_gradients = [leftover_portion - effective for leftover_portion in beside_all]
    bernoulli_coefficients = [bernoulli(voltage_gradient) for voltage_gradient in voltage_gradients]
    denominator_quantity = annihilation_coefficient
    for bernoulli_coefficient, voltage_gradient in zip(bernoulli_coefficients, voltage_gradients):
        denominator_quantity = denominator_quantity + (bernoulli_coefficient + voltage_gradient)

    def sweep(beside):
        fraction_top_quantity = creation_amounts
        for bernoulli_coefficient, leftover_portion in zip(bernoulli_coefficients, beside):
            fraction_top_quantity = fraction_top_quantity + bernoulli_coefficient * leftover_portion
        return fraction_top_quantity / denominator_quantity

    electron_concentration = sweep([b[1] for b in beside_both])
    depth = HEAT_SWEEPS
    heat_inputs = jnp.stack([initial_warming, cooling_coefficient])
    n1 = electron_concentration
    lanes = n1.shape[2]
    count = lax.axis_size("slab")
    forward = [(i, i + 1) for i in range(count - 1)]
    backward = [(i + 1, i) for i in range(count - 1)]
    tc = initial_warming.shape[0]

    def packed(layer, rows):
        return jnp.concatenate([layer[0], rows.reshape(-1, lanes)], axis=0)

    low = lax.ppermute(packed(n1[-1:], heat_inputs[:, tc - depth :]), "slab", forward)
    high = lax.ppermute(packed(n1[:1], heat_inputs[:, :depth]), "slab", backward)
    rows_n = n1.shape[1]
    heat_low = low[rows_n:].reshape(heat_inputs[:, :depth].shape)
    heat_high = high[rows_n:].reshape(heat_inputs[:, :depth].shape)
    y_halos = face_halos(n1, (("gy", 1),))[0]
    electron_concentration = sweep(
        neighbours_of(n1, [(low[None, :rows_n], high[None, :rows_n]), y_halos])
    )
    heat_inputs_ext = jnp.concatenate([heat_low, heat_inputs, heat_high], axis=1)
    n_final = electron_concentration
    y_low, y_high = face_halos(n_final, (("gy", 1),))[0]
    zero_x = jnp.zeros_like(n_final[:1])
    beside_final = neighbours_of(n_final, [(zero_x, zero_x), (y_low, y_high)])
    joule_power_input = jnp.zeros_like(n_final)
    for bernoulli_coefficient, voltage_gradient, leftover_portion in zip(
        bernoulli_coefficients, voltage_gradients, beside_final
    ):
        joule_power_input = joule_power_input + voltage_gradient * (
            bernoulli_coefficient * leftover_portion
            - (bernoulli_coefficient + voltage_gradient) * n_final
        )
    joule_power_input = 0.5 * joule_power_input
    up_x, down_x = voltage_gradients[0], voltage_gradients[1]
    bup_x, bdown_x = bernoulli_coefficients[0], bernoulli_coefficients[1]
    heat_left = -0.5 * (down_x[:1] * ((bdown_x[:1] + down_x[:1]) * n_final[:1]))
    heat_right = -0.5 * (up_x[-1:] * ((bup_x[-1:] + up_x[-1:]) * n_final[-1:]))
    heat_ext = jnp.concatenate([heat_left, joule_power_input, heat_right], axis=0)

    padded_first = jnp.pad(restrict_matrix_first, ((1, 1), (1, 1)))
    ratio = slab_cells // 2
    columns_ext = lax.dynamic_slice(
        padded_first, (me * ratio, me * slab_cells), (BAND, slab_cells + 2)
    )
    columns = columns_ext[:, 1 : 1 + slab_cells]
    along_y = jnp.einsum(
        "ty,xyz->xtz", restrict_matrix_second, heat_ext, precision=upper_limit
    )
    chunk_c = restrict_matrix_third.shape[0] // slabs
    padded_third = jnp.pad(restrict_matrix_third, ((depth, depth), (0, 0)))
    third_windows = jnp.stack(
        [padded_third[chunk_c * k : chunk_c * k + chunk_c + 2 * depth] for k in range(slabs)]
    )
    along_z = jnp.einsum("krz,xtz->krtx", third_windows, along_y, precision=upper_limit)
    piece = jnp.einsum("krtx,ax->krta", along_z, columns_ext, precision=upper_limit)
    got = lax.all_to_all(piece, "slab", 0, 0, tiled=False)
    main = got[..., 1 : 1 + ratio]
    zero_row = jnp.zeros_like(got[:1, ..., 0])
    left = jnp.concatenate([got[1:, ..., 0], zero_row], axis=0)
    right = jnp.concatenate([zero_row, got[:-1, ..., ratio + 1]], axis=0)
    main = main.at[..., ratio - 1].add(left)
    main = main.at[..., 0].add(right)
    source_ext = jnp.transpose(main, (1, 2, 0, 3)).reshape(
        main.shape[1], main.shape[2], slabs * ratio
    )

    stacked = jnp.stack([heat_inputs_ext[0], source_ext, 6.0 + heat_inputs_ext[1]])
    depths = (HEAT_SWEEPS, 8)
    gy_count = lax.axis_size("gy")
    gy_forward = [(i, i + 1) for i in range(gy_count - 1)]
    gy_backward = [(i + 1, i) for i in range(gy_count - 1)]
    size = stacked.shape[2]
    low = lax.ppermute(stacked[:, :, size - depths[1] :], "gy", gy_forward)
    high = lax.ppermute(stacked[:, :, : depths[1]], "gy", gy_backward)
    stacked = jnp.concatenate([low, stacked, high], axis=2)
    tc, tb = initial_warming.shape[0], initial_warming.shape[1]
    c_index = lax.broadcasted_iota(jnp.int32, stacked.shape[1:], 0) + (me * tc - depths[0])
    b_index = lax.broadcasted_iota(jnp.int32, stacked.shape[1:], 1) + (
        lax.axis_index("gy") * tb - depths[1]
    )
    inside = (
        (c_index >= 0)
        & (c_index < slabs * tc)
        & (b_index >= 0)
        & (b_index < lax.axis_size("gy") * tb)
    )
    warm = stacked[0]
    source_ext, scale_ext = stacked[1], stacked[2]
    for repeat in range(HEAT_SWEEPS):
        padded = jnp.pad(warm, 1)
        total = source_ext
        for leftover_portion in (
            padded[2:, 1:-1, 1:-1],
            padded[:-2, 1:-1, 1:-1],
            padded[1:-1, 2:, 1:-1],
            padded[1:-1, :-2, 1:-1],
            padded[1:-1, 1:-1, 2:],
            padded[1:-1, 1:-1, :-2],
        ):
            total = total + leftover_portion
        warm = jnp.where(inside, total / scale_ext, 0.0)
    warming_distribution = warm[depths[0] : depths[0] + tc, depths[1] : depths[1] + tb]

    a_count = warming_distribution.shape[2]
    pick = (
        lax.broadcasted_iota(jnp.int32, (slabs, BAND, a_count), 2)
        == lax.broadcasted_iota(jnp.int32, (slabs, BAND, a_count), 0) * ratio
        + lax.broadcasted_iota(jnp.int32, (slabs, BAND, a_count), 1)
        - 1
    ).astype(jnp.float32)
    windows = jnp.einsum("ska,cba->skcb", pick, warming_distribution, precision=upper_limit)
    got_warm = lax.all_to_all(windows, "slab", 0, 0, tiled=False)
    spread = jnp.einsum("skcb,kx->scbx", got_warm, columns, precision=upper_limit)
    third = restrict_matrix_third.reshape(slabs, chunk_c, restrict_matrix_third.shape[1])
    raised_field = jnp.einsum("scbx,scz->xbz", spread, third, precision=upper_limit)
    fine_mesh_warming = 16.0 * jnp.einsum(
        "hc,qhk->qck", restrict_matrix_second, raised_field, precision=upper_limit
    )
    return (electron_concentration, warming_distribution, fine_mesh_warming)


def solution(mesh):
    in_specs = (
        P("slab", "gy", None),
        P("slab", "gy", None),
        P("slab", "gy", None),
        P("slab", "gy", None),
        P("slab", "gy", None),
        P(),
        P(),
        P("gy", None),
        P(),
        P("slab", "gy", None),
        P("slab", "gy", None),
    )
    out_specs = (P("slab", "gy", None), P("slab", "gy", None), P("slab", "gy", None))
    return jax.shard_map(
        per_device, mesh=mesh, in_specs=in_specs, out_specs=out_specs, check_vma=False
    )
```

```python
import jax
import jax.numpy as jnp
from jax import lax
from jax.sharding import PartitionSpec as P

GRAINS = 4
HEAT_SWEEPS = 3
BAND = 6


def face_halos(block, sides):
    halos = []
    for axis, dim in sides:
        count = lax.axis_size(axis)
        forward = [(i, i + 1) for i in range(count - 1)]
        backward = [(i + 1, i) for i in range(count - 1)]
        size = block.shape[dim]
        low = lax.ppermute(lax.slice_in_dim(block, size - 1, size, axis=dim), axis, forward)
        high = lax.ppermute(lax.slice_in_dim(block, 0, 1, axis=dim), axis, backward)
        halos.append((low, high))
    return halos


def neighbours_of(block, halos, lead=0):
    out = []
    for k, (low, high) in enumerate(halos):
        dim = lead + k
        size = block.shape[dim]
        out.append(jnp.concatenate([lax.slice_in_dim(block, 1, size, axis=dim), high], axis=dim))
        out.append(jnp.concatenate([low, lax.slice_in_dim(block, 0, size - 1, axis=dim)], axis=dim))
    last = block.ndim - 1
    size = block.shape[last]
    zero = jnp.zeros_like(lax.slice_in_dim(block, 0, 1, axis=last))
    out.append(jnp.concatenate([lax.slice_in_dim(block, 1, size, axis=last), zero], axis=last))
    out.append(jnp.concatenate([zero, lax.slice_in_dim(block, 0, size - 1, axis=last)], axis=last))
    return out


def bernoulli(value):
    small = jnp.abs(value) < 0.0001
    safe = jnp.where(small, jnp.float32(1.0), value)
    return jnp.where(small, 1.0 - 0.5 * value, safe / (jnp.exp(safe) - 1.0))


def per_device(
    electrostatic_voltages,
    initial_electrons,
    creation_amounts,
    annihilation_coefficient,
    crystal_orientation_class,
    crystal_barrier_shift,
    restrict_matrix_first,
    restrict_matrix_second,
    restrict_matrix_third,
    cooling_coefficient,
    initial_warming,
):
    upper_limit = lax.Precision.HIGHEST
    slab_cells = electrostatic_voltages.shape[0]
    slabs = lax.axis_size("slab")
    me = lax.axis_index("slab")
    effective = electrostatic_voltages
    for grain in range(GRAINS):
        effective = effective + jnp.where(
            crystal_orientation_class == grain, crystal_barrier_shift[grain], jnp.float32(0.0)
        )
    device_sides = (("slab", 0), ("gy", 1))
    both = jnp.stack([effective, initial_electrons])
    both_halos = face_halos(both, (("slab", 1), ("gy", 2)))
    beside_both = neighbours_of(both, both_halos, lead=1)
    beside_all = [b[0] for b in beside_both]
    voltage_gradients = [leftover_portion - effective for leftover_portion in beside_all]
    bernoulli_coefficients = [bernoulli(voltage_gradient) for voltage_gradient in voltage_gradients]
    denominator_quantity = annihilation_coefficient
    for bernoulli_coefficient, voltage_gradient in zip(bernoulli_coefficients, voltage_gradients):
        denominator_quantity = denominator_quantity + (bernoulli_coefficient + voltage_gradient)

    def sweep(beside):
        fraction_top_quantity = creation_amounts
        for bernoulli_coefficient, leftover_portion in zip(bernoulli_coefficients, beside):
            fraction_top_quantity = fraction_top_quantity + bernoulli_coefficient * leftover_portion
        return fraction_top_quantity / denominator_quantity

    electron_concentration = sweep([b[1] for b in beside_both])
    electron_concentration = sweep(
        neighbours_of(electron_concentration, face_halos(electron_concentration, device_sides))
    )
    n_final = electron_concentration
    y_low, y_high = face_halos(n_final, (("gy", 1),))[0]
    zero_x = jnp.zeros_like(n_final[:1])
    beside_final = neighbours_of(n_final, [(zero_x, zero_x), (y_low, y_high)])
    joule_power_input = jnp.zeros_like(n_final)
    for bernoulli_coefficient, voltage_gradient, leftover_portion in zip(
        bernoulli_coefficients, voltage_gradients, beside_final
    ):
        joule_power_input = joule_power_input + voltage_gradient * (
            bernoulli_coefficient * leftover_portion
            - (bernoulli_coefficient + voltage_gradient) * n_final
        )
    joule_power_input = 0.5 * joule_power_input
    up_x, down_x = voltage_gradients[0], voltage_gradients[1]
    bup_x, bdown_x = bernoulli_coefficients[0], bernoulli_coefficients[1]
    heat_left = -0.5 * (down_x[:1] * ((bdown_x[:1] + down_x[:1]) * n_final[:1]))
    heat_right = -0.5 * (up_x[-1:] * ((bup_x[-1:] + up_x[-1:]) * n_final[-1:]))
    heat_ext = jnp.concatenate([heat_left, joule_power_input, heat_right], axis=0)

    padded_first = jnp.pad(restrict_matrix_first, ((1, 1), (1, 1)))
    ratio = slab_cells // 2
    columns_ext = lax.dynamic_slice(
        padded_first, (me * ratio, me * slab_cells), (BAND, slab_cells + 2)
    )
    columns = columns_ext[:, 1 : 1 + slab_cells]
    along_y = jnp.einsum(
        "ty,xyz->xtz", restrict_matrix_second, heat_ext, precision=upper_limit
    )
    along_z = jnp.einsum("cz,xtz->ctx", restrict_matrix_third, along_y, precision=upper_limit)
    piece = jnp.einsum("ctx,ax->cta", along_z, columns_ext, precision=upper_limit)
    chunk_c = piece.shape[0] // slabs
    piece = piece.reshape(slabs, chunk_c, piece.shape[1], BAND)
    got = lax.all_to_all(piece, "slab", 0, 0, tiled=False)
    main = got[..., 1 : 1 + ratio]
    zero_row = jnp.zeros_like(got[:1, ..., 0])
    left = jnp.concatenate([got[1:, ..., 0], zero_row], axis=0)
    right = jnp.concatenate([zero_row, got[:-1, ..., ratio + 1]], axis=0)
    main = main.at[..., ratio - 1].add(left)
    main = main.at[..., 0].add(right)
    source = jnp.transpose(main, (1, 2, 0, 3)).reshape(chunk_c, main.shape[2], slabs * ratio)

    stacked = jnp.stack([initial_warming, source, 6.0 + cooling_coefficient])
    depths = (HEAT_SWEEPS, 8)
    for (axis, dim), depth in zip((("slab", 1), ("gy", 2)), depths):
        count = lax.axis_size(axis)
        forward = [(i, i + 1) for i in range(count - 1)]
        backward = [(i + 1, i) for i in range(count - 1)]
        size = stacked.shape[dim]
        low = lax.ppermute(lax.slice_in_dim(stacked, size - depth, size, axis=dim), axis, forward)
        high = lax.ppermute(lax.slice_in_dim(stacked, 0, depth, axis=dim), axis, backward)
        stacked = jnp.concatenate([low, stacked, high], axis=dim)
    tc, tb = initial_warming.shape[0], initial_warming.shape[1]
    c_index = lax.broadcasted_iota(jnp.int32, stacked.shape[1:], 0) + (me * tc - depths[0])
    b_index = lax.broadcasted_iota(jnp.int32, stacked.shape[1:], 1) + (
        lax.axis_index("gy") * tb - depths[1]
    )
    inside = (
        (c_index >= 0)
        & (c_index < slabs * tc)
        & (b_index >= 0)
        & (b_index < lax.axis_size("gy") * tb)
    )
    warm = stacked[0]
    source_ext, scale_ext = stacked[1], stacked[2]
    for repeat in range(HEAT_SWEEPS):
        padded = jnp.pad(warm, 1)
        total = source_ext
        for leftover_portion in (
            padded[2:, 1:-1, 1:-1],
            padded[:-2, 1:-1, 1:-1],
            padded[1:-1, 2:, 1:-1],
            padded[1:-1, :-2, 1:-1],
            padded[1:-1, 1:-1, 2:],
            padded[1:-1, 1:-1, :-2],
        ):
            total = total + leftover_portion
        warm = jnp.where(inside, total / scale_ext, 0.0)
    warming_distribution = warm[depths[0] : depths[0] + tc, depths[1] : depths[1] + tb]

    a_count = warming_distribution.shape[2]
    pick = (
        lax.broadcasted_iota(jnp.int32, (slabs, BAND, a_count), 2)
        == lax.broadcasted_iota(jnp.int32, (slabs, BAND, a_count), 0) * ratio
        + lax.broadcasted_iota(jnp.int32, (slabs, BAND, a_count), 1)
        - 1
    ).astype(jnp.float32)
    windows = jnp.einsum("ska,cba->skcb", pick, warming_distribution, precision=upper_limit)
    got_warm = lax.all_to_all(windows, "slab", 0, 0, tiled=False)
    spread = jnp.einsum("skcb,kx->scbx", got_warm, columns, precision=upper_limit)
    third = restrict_matrix_third.reshape(slabs, chunk_c, restrict_matrix_third.shape[1])
    raised_field = jnp.einsum("scbx,scz->xbz", spread, third, precision=upper_limit)
    fine_mesh_warming = 16.0 * jnp.einsum(
        "hc,qhk->qck", restrict_matrix_second, raised_field, precision=upper_limit
    )
    return (electron_concentration, warming_distribution, fine_mesh_warming)


def solution(mesh):
    in_specs = (
        P("slab", "gy", None),
        P("slab", "gy", None),
        P("slab", "gy", None),
        P("slab", "gy", None),
        P("slab", "gy", None),
        P(),
        P(),
        P("gy", None),
        P(),
        P("slab", "gy", None),
        P("slab", "gy", None),
    )
    out_specs = (P("slab", "gy", None), P("slab", "gy", None), P("slab", "gy", None))
    return jax.shard_map(
        per_device, mesh=mesh, in_specs=in_specs, out_specs=out_specs, check_vma=False
    )
```

```python
import jax
import jax.numpy as jnp
from jax import lax
from jax.sharding import PartitionSpec as P

GRAINS = 4
HEAT_SWEEPS = 3
BAND = 6


def face_halos(block, sides):
    halos = []
    for axis, dim in sides:
        count = lax.axis_size(axis)
        forward = [(i, i + 1) for i in range(count - 1)]
        backward = [(i + 1, i) for i in range(count - 1)]
        size = block.shape[dim]
        low = lax.ppermute(lax.slice_in_dim(block, size - 1, size, axis=dim), axis, forward)
        high = lax.ppermute(lax.slice_in_dim(block, 0, 1, axis=dim), axis, backward)
        halos.append((low, high))
    return halos


def neighbours_of(block, halos, lead=0):
    out = []
    for k, (low, high) in enumerate(halos):
        dim = lead + k
        size = block.shape[dim]
        out.append(jnp.concatenate([lax.slice_in_dim(block, 1, size, axis=dim), high], axis=dim))
        out.append(jnp.concatenate([low, lax.slice_in_dim(block, 0, size - 1, axis=dim)], axis=dim))
    last = block.ndim - 1
    size = block.shape[last]
    zero = jnp.zeros_like(lax.slice_in_dim(block, 0, 1, axis=last))
    out.append(jnp.concatenate([lax.slice_in_dim(block, 1, size, axis=last), zero], axis=last))
    out.append(jnp.concatenate([zero, lax.slice_in_dim(block, 0, size - 1, axis=last)], axis=last))
    return out


def bernoulli(value):
    small = jnp.abs(value) < 0.0001
    safe = jnp.where(small, jnp.float32(1.0), value)
    return jnp.where(small, 1.0 - 0.5 * value, safe / (jnp.exp(safe) - 1.0))


def per_device(
    electrostatic_voltages,
    initial_electrons,
    creation_amounts,
    annihilation_coefficient,
    crystal_orientation_class,
    crystal_barrier_shift,
    restrict_matrix_first,
    restrict_matrix_second,
    restrict_matrix_third,
    cooling_coefficient,
    initial_warming,
):
    upper_limit = lax.Precision.HIGHEST
    slab_cells = electrostatic_voltages.shape[0]
    slabs = lax.axis_size("slab")
    me = lax.axis_index("slab")
    effective = electrostatic_voltages
    for grain in range(GRAINS):
        effective = effective + jnp.where(
            crystal_orientation_class == grain, crystal_barrier_shift[grain], jnp.float32(0.0)
        )
    device_sides = (("slab", 0), ("gy", 1))
    both = jnp.stack([effective, initial_electrons])
    both_halos = face_halos(both, (("slab", 1), ("gy", 2)))
    beside_both = neighbours_of(both, both_halos, lead=1)
    beside_all = [b[0] for b in beside_both]
    voltage_gradients = [leftover_portion - effective for leftover_portion in beside_all]
    bernoulli_coefficients = [bernoulli(voltage_gradient) for voltage_gradient in voltage_gradients]
    denominator_quantity = annihilation_coefficient
    for bernoulli_coefficient, voltage_gradient in zip(bernoulli_coefficients, voltage_gradients):
        denominator_quantity = denominator_quantity + (bernoulli_coefficient + voltage_gradient)

    def sweep(beside):
        fraction_top_quantity = creation_amounts
        for bernoulli_coefficient, leftover_portion in zip(bernoulli_coefficients, beside):
            fraction_top_quantity = fraction_top_quantity + bernoulli_coefficient * leftover_portion
        return fraction_top_quantity / denominator_quantity

    electron_concentration = sweep([b[1] for b in beside_both])
    electron_concentration = sweep(
        neighbours_of(electron_concentration, face_halos(electron_concentration, device_sides))
    )
    n_final = electron_concentration
    y_low, y_high = face_halos(n_final, (("gy", 1),))[0]
    zero_x = jnp.zeros_like(n_final[:1])
    beside_final = neighbours_of(n_final, [(zero_x, zero_x), (y_low, y_high)])
    joule_power_input = jnp.zeros_like(n_final)
    for bernoulli_coefficient, voltage_gradient, leftover_portion in zip(
        bernoulli_coefficients, voltage_gradients, beside_final
    ):
        joule_power_input = joule_power_input + voltage_gradient * (
            bernoulli_coefficient * leftover_portion
            - (bernoulli_coefficient + voltage_gradient) * n_final
        )
    joule_power_input = 0.5 * joule_power_input
    down_x = voltage_gradients[1][:1]
    up_x = voltage_gradients[0][-1:]
    heat_left = -0.5 * (down_x * ((bernoulli(down_x) + down_x) * n_final[:1]))
    heat_right = -0.5 * (up_x * ((bernoulli(up_x) + up_x) * n_final[-1:]))
    heat_ext = jnp.concatenate([heat_left, joule_power_input, heat_right], axis=0)

    padded_first = jnp.pad(restrict_matrix_first, ((1, 1), (1, 1)))
    ratio = slab_cells // 2
    columns_ext = lax.dynamic_slice(
        padded_first, (me * ratio, me * slab_cells), (BAND, slab_cells + 2)
    )
    columns = columns_ext[:, 1 : 1 + slab_cells]
    along_y = jnp.einsum(
        "ty,xyz->xtz", restrict_matrix_second, heat_ext, precision=upper_limit
    )
    along_z = jnp.einsum("cz,xtz->ctx", restrict_matrix_third, along_y, precision=upper_limit)
    piece = jnp.einsum("ctx,ax->cta", along_z, columns_ext, precision=upper_limit)
    chunk_c = piece.shape[0] // slabs
    piece = piece.reshape(slabs, chunk_c, piece.shape[1], BAND)
    got = lax.all_to_all(piece, "slab", 0, 0, tiled=False)
    main = got[..., 1 : 1 + ratio]
    zero_row = jnp.zeros_like(got[:1, ..., 0])
    left = jnp.concatenate([got[1:, ..., 0], zero_row], axis=0)
    right = jnp.concatenate([zero_row, got[:-1, ..., ratio + 1]], axis=0)
    main = main.at[..., ratio - 1].add(left)
    main = main.at[..., 0].add(right)
    source = jnp.transpose(main, (1, 2, 0, 3)).reshape(chunk_c, main.shape[2], slabs * ratio)

    stacked = jnp.stack([initial_warming, source, 6.0 + cooling_coefficient])
    depths = (HEAT_SWEEPS, 8)
    for (axis, dim), depth in zip((("slab", 1), ("gy", 2)), depths):
        count = lax.axis_size(axis)
        forward = [(i, i + 1) for i in range(count - 1)]
        backward = [(i + 1, i) for i in range(count - 1)]
        size = stacked.shape[dim]
        low = lax.ppermute(lax.slice_in_dim(stacked, size - depth, size, axis=dim), axis, forward)
        high = lax.ppermute(lax.slice_in_dim(stacked, 0, depth, axis=dim), axis, backward)
        stacked = jnp.concatenate([low, stacked, high], axis=dim)
    tc, tb = initial_warming.shape[0], initial_warming.shape[1]
    c_index = lax.broadcasted_iota(jnp.int32, stacked.shape[1:], 0) + (me * tc - depths[0])
    b_index = lax.broadcasted_iota(jnp.int32, stacked.shape[1:], 1) + (
        lax.axis_index("gy") * tb - depths[1]
    )
    inside = (
        (c_index >= 0)
        & (c_index < slabs * tc)
        & (b_index >= 0)
        & (b_index < lax.axis_size("gy") * tb)
    )
    warm = stacked[0]
    source_ext, scale_ext = stacked[1], stacked[2]
    for repeat in range(HEAT_SWEEPS):
        padded = jnp.pad(warm, 1)
        total = source_ext
        for leftover_portion in (
            padded[2:, 1:-1, 1:-1],
            padded[:-2, 1:-1, 1:-1],
            padded[1:-1, 2:, 1:-1],
            padded[1:-1, :-2, 1:-1],
            padded[1:-1, 1:-1, 2:],
            padded[1:-1, 1:-1, :-2],
        ):
            total = total + leftover_portion
        warm = jnp.where(inside, total / scale_ext, 0.0)
    warming_distribution = warm[depths[0] : depths[0] + tc, depths[1] : depths[1] + tb]

    a_count = warming_distribution.shape[2]
    pick = (
        lax.broadcasted_iota(jnp.int32, (slabs, BAND, a_count), 2)
        == lax.broadcasted_iota(jnp.int32, (slabs, BAND, a_count), 0) * ratio
        + lax.broadcasted_iota(jnp.int32, (slabs, BAND, a_count), 1)
        - 1
    ).astype(jnp.float32)
    windows = jnp.einsum("ska,cba->skcb", pick, warming_distribution, precision=upper_limit)
    got_warm = lax.all_to_all(windows, "slab", 0, 0, tiled=False)
    spread = jnp.einsum("skcb,kx->scbx", got_warm, columns, precision=upper_limit)
    third = restrict_matrix_third.reshape(slabs, chunk_c, restrict_matrix_third.shape[1])
    raised_field = jnp.einsum("scbx,scz->xbz", spread, third, precision=upper_limit)
    fine_mesh_warming = 16.0 * jnp.einsum(
        "hc,qhk->qck", restrict_matrix_second, raised_field, precision=upper_limit
    )
    return (electron_concentration, warming_distribution, fine_mesh_warming)


def solution(mesh):
    in_specs = (
        P("slab", "gy", None),
        P("slab", "gy", None),
        P("slab", "gy", None),
        P("slab", "gy", None),
        P("slab", "gy", None),
        P(),
        P(),
        P("gy", None),
        P(),
        P("slab", "gy", None),
        P("slab", "gy", None),
    )
    out_specs = (P("slab", "gy", None), P("slab", "gy", None), P("slab", "gy", None))
    return jax.shard_map(
        per_device, mesh=mesh, in_specs=in_specs, out_specs=out_specs, check_vma=False
    )
```

```python
import jax
import jax.numpy as jnp
from jax import lax
from jax.sharding import PartitionSpec as P

GRAINS = 4
HEAT_SWEEPS = 3
BAND = 6


def face_halos(block, sides):
    halos = []
    for axis, dim in sides:
        count = lax.axis_size(axis)
        forward = [(i, i + 1) for i in range(count - 1)]
        backward = [(i + 1, i) for i in range(count - 1)]
        size = block.shape[dim]
        low = lax.ppermute(lax.slice_in_dim(block, size - 1, size, axis=dim), axis, forward)
        high = lax.ppermute(lax.slice_in_dim(block, 0, 1, axis=dim), axis, backward)
        halos.append((low, high))
    return halos


def neighbours_of(block, halos, lead=0):
    out = []
    for k, (low, high) in enumerate(halos):
        dim = lead + k
        size = block.shape[dim]
        out.append(jnp.concatenate([lax.slice_in_dim(block, 1, size, axis=dim), high], axis=dim))
        out.append(jnp.concatenate([low, lax.slice_in_dim(block, 0, size - 1, axis=dim)], axis=dim))
    last = block.ndim - 1
    size = block.shape[last]
    zero = jnp.zeros_like(lax.slice_in_dim(block, 0, 1, axis=last))
    out.append(jnp.concatenate([lax.slice_in_dim(block, 1, size, axis=last), zero], axis=last))
    out.append(jnp.concatenate([zero, lax.slice_in_dim(block, 0, size - 1, axis=last)], axis=last))
    return out


def bernoulli(value):
    small = jnp.abs(value) < 0.0001
    safe = jnp.where(small, jnp.float32(1.0), value)
    return jnp.where(small, 1.0 - 0.5 * value, safe / (jnp.exp(safe) - 1.0))


def per_device(
    electrostatic_voltages,
    initial_electrons,
    creation_amounts,
    annihilation_coefficient,
    crystal_orientation_class,
    crystal_barrier_shift,
    restrict_matrix_first,
    restrict_matrix_second,
    restrict_matrix_third,
    cooling_coefficient,
    initial_warming,
):
    upper_limit = lax.Precision.HIGHEST
    slab_cells = electrostatic_voltages.shape[0]
    slabs = lax.axis_size("slab")
    me = lax.axis_index("slab")
    effective = electrostatic_voltages
    for grain in range(GRAINS):
        effective = effective + jnp.where(
            crystal_orientation_class == grain, crystal_barrier_shift[grain], jnp.float32(0.0)
        )
    device_sides = (("slab", 0), ("gy", 1))
    both = jnp.stack([effective, initial_electrons])
    both_halos = face_halos(both, (("slab", 1), ("gy", 2)))
    beside_both = neighbours_of(both, both_halos, lead=1)
    beside_all = [b[0] for b in beside_both]
    voltage_gradients = [leftover_portion - effective for leftover_portion in beside_all]
    bernoulli_coefficients = [bernoulli(voltage_gradient) for voltage_gradient in voltage_gradients]
    denominator_quantity = annihilation_coefficient
    for bernoulli_coefficient, voltage_gradient in zip(bernoulli_coefficients, voltage_gradients):
        denominator_quantity = denominator_quantity + (bernoulli_coefficient + voltage_gradient)

    def sweep(beside):
        fraction_top_quantity = creation_amounts
        for bernoulli_coefficient, leftover_portion in zip(bernoulli_coefficients, beside):
            fraction_top_quantity = fraction_top_quantity + bernoulli_coefficient * leftover_portion
        return fraction_top_quantity / denominator_quantity

    electron_concentration = sweep([b[1] for b in beside_both])
    electron_concentration = sweep(
        neighbours_of(electron_concentration, face_halos(electron_concentration, device_sides))
    )
    n_final = electron_concentration
    y_low, y_high = face_halos(n_final, (("gy", 1),))[0]
    zero_x = jnp.zeros_like(n_final[:1])
    beside_final = neighbours_of(n_final, [(zero_x, zero_x), (y_low, y_high)])
    joule_power_input = jnp.zeros_like(n_final)
    for bernoulli_coefficient, voltage_gradient, leftover_portion in zip(
        bernoulli_coefficients, voltage_gradients, beside_final
    ):
        joule_power_input = joule_power_input + voltage_gradient * (
            bernoulli_coefficient * leftover_portion
            - (bernoulli_coefficient + voltage_gradient) * n_final
        )
    joule_power_input = 0.5 * joule_power_input
    down_x = voltage_gradients[1][:1]
    up_x = voltage_gradients[0][-1:]
    heat_left = -0.5 * (down_x * ((bernoulli(down_x) + down_x) * n_final[:1]))
    heat_right = -0.5 * (up_x * ((bernoulli(up_x) + up_x) * n_final[-1:]))
    heat_ext = jnp.concatenate([heat_left, joule_power_input, heat_right], axis=0)

    padded_first = jnp.pad(restrict_matrix_first, ((1, 1), (1, 1)))
    ratio = slab_cells // 2
    columns_ext = lax.dynamic_slice(
        padded_first, (me * ratio, me * slab_cells), (BAND, slab_cells + 2)
    )
    columns = columns_ext[:, 1 : 1 + slab_cells]
    along_y = jnp.einsum(
        "ty,xyz->xtz", restrict_matrix_second, heat_ext, precision=upper_limit
    )
    along_z = jnp.einsum("cz,xtz->ctx", restrict_matrix_third, along_y, precision=upper_limit)
    piece = jnp.einsum("ctx,ax->cta", along_z, columns_ext, precision=upper_limit)
    chunk_c = piece.shape[0] // slabs
    piece = piece.reshape(slabs, chunk_c, piece.shape[1], BAND)
    got = lax.all_to_all(piece, "slab", 0, 0, tiled=False)
    main = got[..., 1 : 1 + ratio]
    zero_row = jnp.zeros_like(got[:1, ..., 0])
    left = jnp.concatenate([got[1:, ..., 0], zero_row], axis=0)
    right = jnp.concatenate([zero_row, got[:-1, ..., ratio + 1]], axis=0)
    main = main.at[..., ratio - 1].add(left)
    main = main.at[..., 0].add(right)
    source = jnp.transpose(main, (1, 2, 0, 3)).reshape(chunk_c, main.shape[2], slabs * ratio)

    stacked = jnp.stack([initial_warming, source, 6.0 + cooling_coefficient])
    depths = (HEAT_SWEEPS, 8)
    for (axis, dim), depth in zip((("slab", 1), ("gy", 2)), depths):
        count = lax.axis_size(axis)
        forward = [(i, i + 1) for i in range(count - 1)]
        backward = [(i + 1, i) for i in range(count - 1)]
        size = stacked.shape[dim]
        low = lax.ppermute(lax.slice_in_dim(stacked, size - depth, size, axis=dim), axis, forward)
        high = lax.ppermute(lax.slice_in_dim(stacked, 0, depth, axis=dim), axis, backward)
        stacked = jnp.concatenate([low, stacked, high], axis=dim)
    tc, tb = initial_warming.shape[0], initial_warming.shape[1]
    c_index = lax.broadcasted_iota(jnp.int32, stacked.shape[1:], 0) + (me * tc - depths[0])
    b_index = lax.broadcasted_iota(jnp.int32, stacked.shape[1:], 1) + (
        lax.axis_index("gy") * tb - depths[1]
    )
    inside = (
        (c_index >= 0)
        & (c_index < slabs * tc)
        & (b_index >= 0)
        & (b_index < lax.axis_size("gy") * tb)
    )
    warm = stacked[0]
    source_ext, scale_ext = stacked[1], stacked[2]
    for repeat in range(HEAT_SWEEPS):
        padded = jnp.pad(warm, 1)
        total = source_ext
        for leftover_portion in (
            padded[2:, 1:-1, 1:-1],
            padded[:-2, 1:-1, 1:-1],
            padded[1:-1, 2:, 1:-1],
            padded[1:-1, :-2, 1:-1],
            padded[1:-1, 1:-1, 2:],
            padded[1:-1, 1:-1, :-2],
        ):
            total = total + leftover_portion
        warm = jnp.where(inside, total / scale_ext, 0.0)
    warming_distribution = warm[depths[0] : depths[0] + tc, depths[1] : depths[1] + tb]

    a_count = warming_distribution.shape[2]
    pick = (
        lax.broadcasted_iota(jnp.int32, (slabs, BAND, a_count), 2)
        == lax.broadcasted_iota(jnp.int32, (slabs, BAND, a_count), 0) * ratio
        + lax.broadcasted_iota(jnp.int32, (slabs, BAND, a_count), 1)
        - 1
    ).astype(jnp.float32)
    windows = jnp.einsum("ska,cba->skcb", pick, warming_distribution, precision=upper_limit)
    got_warm = lax.all_to_all(windows, "slab", 0, 0, tiled=False)
    spread = jnp.einsum("skcb,kx->scbx", got_warm, columns, precision=upper_limit)
    third = restrict_matrix_third.reshape(slabs, chunk_c, restrict_matrix_third.shape[1])
    spread_y = jnp.einsum("scbx,by->scxy", spread, restrict_matrix_second, precision=upper_limit)
    fine_mesh_warming = 16.0 * jnp.einsum(
        "scxy,scz->xyz", spread_y, third, precision=upper_limit
    )
    return (electron_concentration, warming_distribution, fine_mesh_warming)


def solution(mesh):
    in_specs = (
        P("slab", "gy", None),
        P("slab", "gy", None),
        P("slab", "gy", None),
        P("slab", "gy", None),
        P("slab", "gy", None),
        P(),
        P(),
        P("gy", None),
        P(),
        P("slab", "gy", None),
        P("slab", "gy", None),
    )
    out_specs = (P("slab", "gy", None), P("slab", "gy", None), P("slab", "gy", None))
    return jax.shard_map(
        per_device, mesh=mesh, in_specs=in_specs, out_specs=out_specs, check_vma=False
    )
```

```python
import jax
import jax.numpy as jnp
from jax import lax
from jax.sharding import PartitionSpec as P

GRAINS = 4
HEAT_SWEEPS = 3
BAND = 6


def face_halos(block, sides):
    halos = []
    for axis, dim in sides:
        count = lax.axis_size(axis)
        forward = [(i, i + 1) for i in range(count - 1)]
        backward = [(i + 1, i) for i in range(count - 1)]
        size = block.shape[dim]
        low = lax.ppermute(lax.slice_in_dim(block, size - 1, size, axis=dim), axis, forward)
        high = lax.ppermute(lax.slice_in_dim(block, 0, 1, axis=dim), axis, backward)
        halos.append((low, high))
    return halos


def neighbours_of(block, halos, lead=0):
    out = []
    for k, (low, high) in enumerate(halos):
        dim = lead + k
        size = block.shape[dim]
        out.append(jnp.concatenate([lax.slice_in_dim(block, 1, size, axis=dim), high], axis=dim))
        out.append(jnp.concatenate([low, lax.slice_in_dim(block, 0, size - 1, axis=dim)], axis=dim))
    last = block.ndim - 1
    size = block.shape[last]
    zero = jnp.zeros_like(lax.slice_in_dim(block, 0, 1, axis=last))
    out.append(jnp.concatenate([lax.slice_in_dim(block, 1, size, axis=last), zero], axis=last))
    out.append(jnp.concatenate([zero, lax.slice_in_dim(block, 0, size - 1, axis=last)], axis=last))
    return out


def bernoulli(value):
    small = jnp.abs(value) < 0.0001
    safe = jnp.where(small, jnp.float32(1.0), value)
    return jnp.where(small, 1.0 - 0.5 * value, safe / (jnp.exp(safe) - 1.0))


def per_device(
    electrostatic_voltages,
    initial_electrons,
    creation_amounts,
    annihilation_coefficient,
    crystal_orientation_class,
    crystal_barrier_shift,
    restrict_matrix_first,
    restrict_matrix_second,
    restrict_matrix_third,
    cooling_coefficient,
    initial_warming,
):
    upper_limit = lax.Precision.HIGHEST
    slab_cells = electrostatic_voltages.shape[0]
    slabs = lax.axis_size("slab")
    me = lax.axis_index("slab")
    effective = electrostatic_voltages
    for grain in range(GRAINS):
        effective = effective + jnp.where(
            crystal_orientation_class == grain, crystal_barrier_shift[grain], jnp.float32(0.0)
        )
    device_sides = (("slab", 0), ("gy", 1))
    both = jnp.stack([effective, initial_electrons])
    both_halos = face_halos(both, (("slab", 1), ("gy", 2)))
    beside_both = neighbours_of(both, both_halos, lead=1)
    beside_all = [b[0] for b in beside_both]
    voltage_gradients = [leftover_portion - effective for leftover_portion in beside_all]
    bernoulli_coefficients = [bernoulli(voltage_gradient) for voltage_gradient in voltage_gradients]
    start_beside = [b[1] for b in beside_both]
    partial_denominator = annihilation_coefficient
    partial_top = creation_amounts
    for d in (2, 3, 4, 5):
        partial_denominator = partial_denominator + (
            bernoulli_coefficients[d] + voltage_gradients[d]
        )
        partial_top = partial_top + bernoulli_coefficients[d] * start_beside[d]
    partial_denominator, partial_top = lax.optimization_barrier(
        (partial_denominator, partial_top)
    )
    denominator_quantity = partial_denominator
    for d in (0, 1):
        denominator_quantity = denominator_quantity + (
            bernoulli_coefficients[d] + voltage_gradients[d]
        )
        partial_top = partial_top + bernoulli_coefficients[d] * start_beside[d]

    def sweep(beside):
        fraction_top_quantity = creation_amounts
        for bernoulli_coefficient, leftover_portion in zip(bernoulli_coefficients, beside):
            fraction_top_quantity = fraction_top_quantity + bernoulli_coefficient * leftover_portion
        return fraction_top_quantity / denominator_quantity

    electron_concentration = partial_top / denominator_quantity
    electron_concentration = sweep(
        neighbours_of(electron_concentration, face_halos(electron_concentration, device_sides))
    )
    n_final = electron_concentration
    y_low, y_high = face_halos(n_final, (("gy", 1),))[0]
    zero_x = jnp.zeros_like(n_final[:1])
    beside_final = neighbours_of(n_final, [(zero_x, zero_x), (y_low, y_high)])
    joule_power_input = jnp.zeros_like(n_final)
    for bernoulli_coefficient, voltage_gradient, leftover_portion in zip(
        bernoulli_coefficients, voltage_gradients, beside_final
    ):
        joule_power_input = joule_power_input + voltage_gradient * (
            bernoulli_coefficient * leftover_portion
            - (bernoulli_coefficient + voltage_gradient) * n_final
        )
    joule_power_input = 0.5 * joule_power_input
    down_x = voltage_gradients[1][:1]
    up_x = voltage_gradients[0][-1:]
    heat_left = -0.5 * (down_x * ((bernoulli(down_x) + down_x) * n_final[:1]))
    heat_right = -0.5 * (up_x * ((bernoulli(up_x) + up_x) * n_final[-1:]))
    heat_ext = jnp.concatenate([heat_left, joule_power_input, heat_right], axis=0)

    padded_first = jnp.pad(restrict_matrix_first, ((1, 1), (1, 1)))
    ratio = slab_cells // 2
    columns_ext = lax.dynamic_slice(
        padded_first, (me * ratio, me * slab_cells), (BAND, slab_cells + 2)
    )
    columns = columns_ext[:, 1 : 1 + slab_cells]
    along_y = jnp.einsum(
        "ty,xyz->xtz", restrict_matrix_second, heat_ext, precision=upper_limit
    )
    along_z = jnp.einsum("cz,xtz->ctx", restrict_matrix_third, along_y, precision=upper_limit)
    piece = jnp.einsum("ctx,ax->cta", along_z, columns_ext, precision=upper_limit)
    chunk_c = piece.shape[0] // slabs
    piece = piece.reshape(slabs, chunk_c, piece.shape[1], BAND)
    got = lax.all_to_all(piece, "slab", 0, 0, tiled=False)
    main = got[..., 1 : 1 + ratio]
    zero_row = jnp.zeros_like(got[:1, ..., 0])
    left = jnp.concatenate([got[1:, ..., 0], zero_row], axis=0)
    right = jnp.concatenate([zero_row, got[:-1, ..., ratio + 1]], axis=0)
    main = main.at[..., ratio - 1].add(left)
    main = main.at[..., 0].add(right)
    source = jnp.transpose(main, (1, 2, 0, 3)).reshape(chunk_c, main.shape[2], slabs * ratio)

    stacked = jnp.stack([initial_warming, source, 6.0 + cooling_coefficient])
    depths = (HEAT_SWEEPS, 8)
    for (axis, dim), depth in zip((("slab", 1), ("gy", 2)), depths):
        count = lax.axis_size(axis)
        forward = [(i, i + 1) for i in range(count - 1)]
        backward = [(i + 1, i) for i in range(count - 1)]
        size = stacked.shape[dim]
        low = lax.ppermute(lax.slice_in_dim(stacked, size - depth, size, axis=dim), axis, forward)
        high = lax.ppermute(lax.slice_in_dim(stacked, 0, depth, axis=dim), axis, backward)
        stacked = jnp.concatenate([low, stacked, high], axis=dim)
    tc, tb = initial_warming.shape[0], initial_warming.shape[1]
    c_index = lax.broadcasted_iota(jnp.int32, stacked.shape[1:], 0) + (me * tc - depths[0])
    b_index = lax.broadcasted_iota(jnp.int32, stacked.shape[1:], 1) + (
        lax.axis_index("gy") * tb - depths[1]
    )
    inside = (
        (c_index >= 0)
        & (c_index < slabs * tc)
        & (b_index >= 0)
        & (b_index < lax.axis_size("gy") * tb)
    )
    warm = stacked[0]
    source_ext, scale_ext = stacked[1], stacked[2]
    for repeat in range(HEAT_SWEEPS):
        padded = jnp.pad(warm, 1)
        total = source_ext
        for leftover_portion in (
            padded[2:, 1:-1, 1:-1],
            padded[:-2, 1:-1, 1:-1],
            padded[1:-1, 2:, 1:-1],
            padded[1:-1, :-2, 1:-1],
            padded[1:-1, 1:-1, 2:],
            padded[1:-1, 1:-1, :-2],
        ):
            total = total + leftover_portion
        warm = jnp.where(inside, total / scale_ext, 0.0)
    warming_distribution = warm[depths[0] : depths[0] + tc, depths[1] : depths[1] + tb]

    a_count = warming_distribution.shape[2]
    pick = (
        lax.broadcasted_iota(jnp.int32, (slabs, BAND, a_count), 2)
        == lax.broadcasted_iota(jnp.int32, (slabs, BAND, a_count), 0) * ratio
        + lax.broadcasted_iota(jnp.int32, (slabs, BAND, a_count), 1)
        - 1
    ).astype(jnp.float32)
    windows = jnp.einsum("ska,cba->skcb", pick, warming_distribution, precision=upper_limit)
    got_warm = lax.all_to_all(windows, "slab", 0, 0, tiled=False)
    spread = jnp.einsum("skcb,kx->scbx", got_warm, columns, precision=upper_limit)
    third = restrict_matrix_third.reshape(slabs, chunk_c, restrict_matrix_third.shape[1])
    spread_y = jnp.einsum("scbx,by->scxy", spread, restrict_matrix_second, precision=upper_limit)
    fine_mesh_warming = 16.0 * jnp.einsum(
        "scxy,scz->xyz", spread_y, third, precision=upper_limit
    )
    return (electron_concentration, warming_distribution, fine_mesh_warming)


def solution(mesh):
    in_specs = (
        P("slab", "gy", None),
        P("slab", "gy", None),
        P("slab", "gy", None),
        P("slab", "gy", None),
        P("slab", "gy", None),
        P(),
        P(),
        P("gy", None),
        P(),
        P("slab", "gy", None),
        P("slab", "gy", None),
    )
    out_specs = (P("slab", "gy", None), P("slab", "gy", None), P("slab", "gy", None))
    return jax.shard_map(
        per_device, mesh=mesh, in_specs=in_specs, out_specs=out_specs, check_vma=False
    )
```

```python
import jax
import jax.numpy as jnp
from jax import lax
from jax.sharding import PartitionSpec as P

GRAINS = 4
HEAT_SWEEPS = 3
BAND = 6


def face_halos(block, sides):
    halos = []
    for axis, dim in sides:
        count = lax.axis_size(axis)
        forward = [(i, i + 1) for i in range(count - 1)]
        backward = [(i + 1, i) for i in range(count - 1)]
        size = block.shape[dim]
        low = lax.ppermute(lax.slice_in_dim(block, size - 1, size, axis=dim), axis, forward)
        high = lax.ppermute(lax.slice_in_dim(block, 0, 1, axis=dim), axis, backward)
        halos.append((low, high))
    return halos


def neighbours_of(block, halos, lead=0):
    out = []
    for k, (low, high) in enumerate(halos):
        dim = lead + k
        size = block.shape[dim]
        out.append(jnp.concatenate([lax.slice_in_dim(block, 1, size, axis=dim), high], axis=dim))
        out.append(jnp.concatenate([low, lax.slice_in_dim(block, 0, size - 1, axis=dim)], axis=dim))
    last = block.ndim - 1
    size = block.shape[last]
    widths = [(0, 0)] * last + [(1, 1)]
    padded = jnp.pad(block, widths)
    out.append(lax.slice_in_dim(padded, 2, size + 2, axis=last))
    out.append(lax.slice_in_dim(padded, 0, size, axis=last))
    return out


def bernoulli(value):
    small = jnp.abs(value) < 0.0001
    safe = jnp.where(small, jnp.float32(1.0), value)
    return jnp.where(small, 1.0 - 0.5 * value, safe / (jnp.exp(safe) - 1.0))


def per_device(
    electrostatic_voltages,
    initial_electrons,
    creation_amounts,
    annihilation_coefficient,
    crystal_orientation_class,
    crystal_barrier_shift,
    restrict_matrix_first,
    restrict_matrix_second,
    restrict_matrix_third,
    cooling_coefficient,
    initial_warming,
):
    upper_limit = lax.Precision.HIGHEST
    slab_cells = electrostatic_voltages.shape[0]
    slabs = lax.axis_size("slab")
    me = lax.axis_index("slab")
    effective = electrostatic_voltages
    for grain in range(GRAINS):
        effective = effective + jnp.where(
            crystal_orientation_class == grain, crystal_barrier_shift[grain], jnp.float32(0.0)
        )
    device_sides = (("slab", 0), ("gy", 1))
    both = jnp.stack([effective, initial_electrons])
    both_halos = face_halos(both, (("slab", 1), ("gy", 2)))
    beside_both = neighbours_of(both, both_halos, lead=1)
    beside_all = [b[0] for b in beside_both]
    voltage_gradients = [leftover_portion - effective for leftover_portion in beside_all]
    bernoulli_coefficients = [bernoulli(voltage_gradient) for voltage_gradient in voltage_gradients]
    denominator_quantity = annihilation_coefficient
    for bernoulli_coefficient, voltage_gradient in zip(bernoulli_coefficients, voltage_gradients):
        denominator_quantity = denominator_quantity + (bernoulli_coefficient + voltage_gradient)

    def sweep(beside):
        fraction_top_quantity = creation_amounts
        for bernoulli_coefficient, leftover_portion in zip(bernoulli_coefficients, beside):
            fraction_top_quantity = fraction_top_quantity + bernoulli_coefficient * leftover_portion
        return fraction_top_quantity / denominator_quantity

    electron_concentration = sweep([b[1] for b in beside_both])
    electron_concentration = sweep(
        neighbours_of(electron_concentration, face_halos(electron_concentration, device_sides))
    )
    n_final = electron_concentration
    y_low, y_high = face_halos(n_final, (("gy", 1),))[0]
    zero_x = jnp.zeros_like(n_final[:1])
    beside_final = neighbours_of(n_final, [(zero_x, zero_x), (y_low, y_high)])
    joule_power_input = jnp.zeros_like(n_final)
    for bernoulli_coefficient, voltage_gradient, leftover_portion in zip(
        bernoulli_coefficients, voltage_gradients, beside_final
    ):
        joule_power_input = joule_power_input + voltage_gradient * (
            bernoulli_coefficient * leftover_portion
            - (bernoulli_coefficient + voltage_gradient) * n_final
        )
    joule_power_input = 0.5 * joule_power_input
    down_x = voltage_gradients[1][:1]
    up_x = voltage_gradients[0][-1:]
    heat_left = -0.5 * (down_x * ((bernoulli(down_x) + down_x) * n_final[:1]))
    heat_right = -0.5 * (up_x * ((bernoulli(up_x) + up_x) * n_final[-1:]))
    heat_ext = jnp.concatenate([heat_left, joule_power_input, heat_right], axis=0)

    padded_first = jnp.pad(restrict_matrix_first, ((1, 1), (1, 1)))
    ratio = slab_cells // 2
    columns_ext = lax.dynamic_slice(
        padded_first, (me * ratio, me * slab_cells), (BAND, slab_cells + 2)
    )
    columns = columns_ext[:, 1 : 1 + slab_cells]
    along_y = jnp.einsum(
        "ty,xyz->xtz", restrict_matrix_second, heat_ext, precision=upper_limit
    )
    along_z = jnp.einsum("cz,xtz->ctx", restrict_matrix_third, along_y, precision=upper_limit)
    piece = jnp.einsum("ctx,ax->cta", along_z, columns_ext, precision=upper_limit)
    chunk_c = piece.shape[0] // slabs
    piece = piece.reshape(slabs, chunk_c, piece.shape[1], BAND)
    got = lax.all_to_all(piece, "slab", 0, 0, tiled=False)
    main = got[..., 1 : 1 + ratio]
    zero_row = jnp.zeros_like(got[:1, ..., 0])
    left = jnp.concatenate([got[1:, ..., 0], zero_row], axis=0)
    right = jnp.concatenate([zero_row, got[:-1, ..., ratio + 1]], axis=0)
    main = main.at[..., ratio - 1].add(left)
    main = main.at[..., 0].add(right)
    source = jnp.transpose(main, (1, 2, 0, 3)).reshape(chunk_c, main.shape[2], slabs * ratio)

    stacked = jnp.stack([initial_warming, source, 6.0 + cooling_coefficient])
    depths = (HEAT_SWEEPS, 8)
    for (axis, dim), depth in zip((("slab", 1), ("gy", 2)), depths):
        count = lax.axis_size(axis)
        forward = [(i, i + 1) for i in range(count - 1)]
        backward = [(i + 1, i) for i in range(count - 1)]
        size = stacked.shape[dim]
        low = lax.ppermute(lax.slice_in_dim(stacked, size - depth, size, axis=dim), axis, forward)
        high = lax.ppermute(lax.slice_in_dim(stacked, 0, depth, axis=dim), axis, backward)
        stacked = jnp.concatenate([low, stacked, high], axis=dim)
    tc, tb = initial_warming.shape[0], initial_warming.shape[1]
    c_index = lax.broadcasted_iota(jnp.int32, stacked.shape[1:], 0) + (me * tc - depths[0])
    b_index = lax.broadcasted_iota(jnp.int32, stacked.shape[1:], 1) + (
        lax.axis_index("gy") * tb - depths[1]
    )
    inside = (
        (c_index >= 0)
        & (c_index < slabs * tc)
        & (b_index >= 0)
        & (b_index < lax.axis_size("gy") * tb)
    )
    warm = stacked[0]
    source_ext, scale_ext = stacked[1], stacked[2]
    for repeat in range(HEAT_SWEEPS):
        padded = jnp.pad(warm, 1)
        total = source_ext
        for leftover_portion in (
            padded[2:, 1:-1, 1:-1],
            padded[:-2, 1:-1, 1:-1],
            padded[1:-1, 2:, 1:-1],
            padded[1:-1, :-2, 1:-1],
            padded[1:-1, 1:-1, 2:],
            padded[1:-1, 1:-1, :-2],
        ):
            total = total + leftover_portion
        warm = jnp.where(inside, total / scale_ext, 0.0)
    warming_distribution = warm[depths[0] : depths[0] + tc, depths[1] : depths[1] + tb]

    a_count = warming_distribution.shape[2]
    pick = (
        lax.broadcasted_iota(jnp.int32, (slabs, BAND, a_count), 2)
        == lax.broadcasted_iota(jnp.int32, (slabs, BAND, a_count), 0) * ratio
        + lax.broadcasted_iota(jnp.int32, (slabs, BAND, a_count), 1)
        - 1
    ).astype(jnp.float32)
    windows = jnp.einsum("ska,cba->skcb", pick, warming_distribution, precision=upper_limit)
    got_warm = lax.all_to_all(windows, "slab", 0, 0, tiled=False)
    spread = jnp.einsum("skcb,kx->scbx", got_warm, columns, precision=upper_limit)
    third = restrict_matrix_third.reshape(slabs, chunk_c, restrict_matrix_third.shape[1])
    spread_y = jnp.einsum("scbx,by->scxy", spread, restrict_matrix_second, precision=upper_limit)
    fine_mesh_warming = 16.0 * jnp.einsum(
        "scxy,scz->xyz", spread_y, third, precision=upper_limit
    )
    return (electron_concentration, warming_distribution, fine_mesh_warming)


def solution(mesh):
    in_specs = (
        P("slab", "gy", None),
        P("slab", "gy", None),
        P("slab", "gy", None),
        P("slab", "gy", None),
        P("slab", "gy", None),
        P(),
        P(),
        P("gy", None),
        P(),
        P("slab", "gy", None),
        P("slab", "gy", None),
    )
    out_specs = (P("slab", "gy", None), P("slab", "gy", None), P("slab", "gy", None))
    return jax.shard_map(
        per_device, mesh=mesh, in_specs=in_specs, out_specs=out_specs, check_vma=False
    )
```

```python
import jax
import jax.numpy as jnp
from jax import lax
from jax.sharding import PartitionSpec as P

GRAINS = 4
HEAT_SWEEPS = 3
BAND = 6


def face_halos(block, sides):
    halos = []
    for axis, dim in sides:
        count = lax.axis_size(axis)
        forward = [(i, i + 1) for i in range(count - 1)]
        backward = [(i + 1, i) for i in range(count - 1)]
        size = block.shape[dim]
        low = lax.ppermute(lax.slice_in_dim(block, size - 1, size, axis=dim), axis, forward)
        high = lax.ppermute(lax.slice_in_dim(block, 0, 1, axis=dim), axis, backward)
        halos.append((low, high))
    return halos


def neighbours_of(block, halos, lead=0):
    out = []
    for k, (low, high) in enumerate(halos):
        dim = lead + k
        size = block.shape[dim]
        out.append(jnp.concatenate([lax.slice_in_dim(block, 1, size, axis=dim), high], axis=dim))
        out.append(jnp.concatenate([low, lax.slice_in_dim(block, 0, size - 1, axis=dim)], axis=dim))
    last = block.ndim - 1
    size = block.shape[last]
    zero = jnp.zeros_like(lax.slice_in_dim(block, 0, 1, axis=last))
    out.append(jnp.concatenate([lax.slice_in_dim(block, 1, size, axis=last), zero], axis=last))
    out.append(jnp.concatenate([zero, lax.slice_in_dim(block, 0, size - 1, axis=last)], axis=last))
    return out


def bernoulli(value):
    small = jnp.abs(value) < 0.0001
    return jnp.where(small, 1.0 - 0.5 * value, value / (jnp.exp(value) - 1.0))


def per_device(
    electrostatic_voltages,
    initial_electrons,
    creation_amounts,
    annihilation_coefficient,
    crystal_orientation_class,
    crystal_barrier_shift,
    restrict_matrix_first,
    restrict_matrix_second,
    restrict_matrix_third,
    cooling_coefficient,
    initial_warming,
):
    upper_limit = lax.Precision.HIGHEST
    slab_cells = electrostatic_voltages.shape[0]
    slabs = lax.axis_size("slab")
    me = lax.axis_index("slab")
    effective = electrostatic_voltages
    for grain in range(GRAINS):
        effective = effective + jnp.where(
            crystal_orientation_class == grain, crystal_barrier_shift[grain], jnp.float32(0.0)
        )
    device_sides = (("slab", 0), ("gy", 1))
    both = jnp.stack([effective, initial_electrons])
    both_halos = face_halos(both, (("slab", 1), ("gy", 2)))
    beside_both = neighbours_of(both, both_halos, lead=1)
    beside_all = [b[0] for b in beside_both]
    voltage_gradients = [leftover_portion - effective for leftover_portion in beside_all]
    bernoulli_coefficients = [bernoulli(voltage_gradient) for voltage_gradient in voltage_gradients]
    denominator_quantity = annihilation_coefficient
    for bernoulli_coefficient, voltage_gradient in zip(bernoulli_coefficients, voltage_gradients):
        denominator_quantity = denominator_quantity + (bernoulli_coefficient + voltage_gradient)

    def sweep(beside):
        fraction_top_quantity = creation_amounts
        for bernoulli_coefficient, leftover_portion in zip(bernoulli_coefficients, beside):
            fraction_top_quantity = fraction_top_quantity + bernoulli_coefficient * leftover_portion
        return fraction_top_quantity / denominator_quantity

    electron_concentration = sweep([b[1] for b in beside_both])
    electron_concentration = sweep(
        neighbours_of(electron_concentration, face_halos(electron_concentration, device_sides))
    )
    n_final = electron_concentration
    y_low, y_high = face_halos(n_final, (("gy", 1),))[0]
    zero_x = jnp.zeros_like(n_final[:1])
    beside_final = neighbours_of(n_final, [(zero_x, zero_x), (y_low, y_high)])
    joule_power_input = jnp.zeros_like(n_final)
    for bernoulli_coefficient, voltage_gradient, leftover_portion in zip(
        bernoulli_coefficients, voltage_gradients, beside_final
    ):
        joule_power_input = joule_power_input + voltage_gradient * (
            bernoulli_coefficient * leftover_portion
            - (bernoulli_coefficient + voltage_gradient) * n_final
        )
    joule_power_input = 0.5 * joule_power_input
    down_x = voltage_gradients[1][:1]
    up_x = voltage_gradients[0][-1:]
    heat_left = -0.5 * (down_x * ((bernoulli(down_x) + down_x) * n_final[:1]))
    heat_right = -0.5 * (up_x * ((bernoulli(up_x) + up_x) * n_final[-1:]))
    heat_ext = jnp.concatenate([heat_left, joule_power_input, heat_right], axis=0)

    padded_first = jnp.pad(restrict_matrix_first, ((1, 1), (1, 1)))
    ratio = slab_cells // 2
    columns_ext = lax.dynamic_slice(
        padded_first, (me * ratio, me * slab_cells), (BAND, slab_cells + 2)
    )
    columns = columns_ext[:, 1 : 1 + slab_cells]
    along_y = jnp.einsum(
        "ty,xyz->xtz", restrict_matrix_second, heat_ext, precision=upper_limit
    )
    along_z = jnp.einsum("cz,xtz->ctx", restrict_matrix_third, along_y, precision=upper_limit)
    piece = jnp.einsum("ctx,ax->cta", along_z, columns_ext, precision=upper_limit)
    chunk_c = piece.shape[0] // slabs
    piece = piece.reshape(slabs, chunk_c, piece.shape[1], BAND)
    got = lax.all_to_all(piece, "slab", 0, 0, tiled=False)
    main = got[..., 1 : 1 + ratio]
    zero_row = jnp.zeros_like(got[:1, ..., 0])
    left = jnp.concatenate([got[1:, ..., 0], zero_row], axis=0)
    right = jnp.concatenate([zero_row, got[:-1, ..., ratio + 1]], axis=0)
    main = main.at[..., ratio - 1].add(left)
    main = main.at[..., 0].add(right)
    source = jnp.transpose(main, (1, 2, 0, 3)).reshape(chunk_c, main.shape[2], slabs * ratio)

    stacked = jnp.stack([initial_warming, source, 6.0 + cooling_coefficient])
    depths = (HEAT_SWEEPS, 8)
    for (axis, dim), depth in zip((("slab", 1), ("gy", 2)), depths):
        count = lax.axis_size(axis)
        forward = [(i, i + 1) for i in range(count - 1)]
        backward = [(i + 1, i) for i in range(count - 1)]
        size = stacked.shape[dim]
        low = lax.ppermute(lax.slice_in_dim(stacked, size - depth, size, axis=dim), axis, forward)
        high = lax.ppermute(lax.slice_in_dim(stacked, 0, depth, axis=dim), axis, backward)
        stacked = jnp.concatenate([low, stacked, high], axis=dim)
    tc, tb = initial_warming.shape[0], initial_warming.shape[1]
    c_index = lax.broadcasted_iota(jnp.int32, stacked.shape[1:], 0) + (me * tc - depths[0])
    b_index = lax.broadcasted_iota(jnp.int32, stacked.shape[1:], 1) + (
        lax.axis_index("gy") * tb - depths[1]
    )
    inside = (
        (c_index >= 0)
        & (c_index < slabs * tc)
        & (b_index >= 0)
        & (b_index < lax.axis_size("gy") * tb)
    )
    warm = stacked[0]
    source_ext, scale_ext = stacked[1], stacked[2]
    for repeat in range(HEAT_SWEEPS):
        padded = jnp.pad(warm, 1)
        total = source_ext
        for leftover_portion in (
            padded[2:, 1:-1, 1:-1],
            padded[:-2, 1:-1, 1:-1],
            padded[1:-1, 2:, 1:-1],
            padded[1:-1, :-2, 1:-1],
            padded[1:-1, 1:-1, 2:],
            padded[1:-1, 1:-1, :-2],
        ):
            total = total + leftover_portion
        warm = jnp.where(inside, total / scale_ext, 0.0)
    warming_distribution = warm[depths[0] : depths[0] + tc, depths[1] : depths[1] + tb]

    a_count = warming_distribution.shape[2]
    pick = (
        lax.broadcasted_iota(jnp.int32, (slabs, BAND, a_count), 2)
        == lax.broadcasted_iota(jnp.int32, (slabs, BAND, a_count), 0) * ratio
        + lax.broadcasted_iota(jnp.int32, (slabs, BAND, a_count), 1)
        - 1
    ).astype(jnp.float32)
    windows = jnp.einsum("ska,cba->skcb", pick, warming_distribution, precision=upper_limit)
    got_warm = lax.all_to_all(windows, "slab", 0, 0, tiled=False)
    spread = jnp.einsum("skcb,kx->scbx", got_warm, columns, precision=upper_limit)
    third = restrict_matrix_third.reshape(slabs, chunk_c, restrict_matrix_third.shape[1])
    spread_y = jnp.einsum("scbx,by->scxy", spread, restrict_matrix_second, precision=upper_limit)
    fine_mesh_warming = 16.0 * jnp.einsum(
        "scxy,scz->xyz", spread_y, third, precision=upper_limit
    )
    return (electron_concentration, warming_distribution, fine_mesh_warming)


def solution(mesh):
    in_specs = (
        P("slab", "gy", None),
        P("slab", "gy", None),
        P("slab", "gy", None),
        P("slab", "gy", None),
        P("slab", "gy", None),
        P(),
        P(),
        P("gy", None),
        P(),
        P("slab", "gy", None),
        P("slab", "gy", None),
    )
    out_specs = (P("slab", "gy", None), P("slab", "gy", None), P("slab", "gy", None))
    return jax.shard_map(
        per_device, mesh=mesh, in_specs=in_specs, out_specs=out_specs, check_vma=False
    )
```

```python
import jax
import jax.numpy as jnp
from jax import lax
from jax.sharding import PartitionSpec as P

GRAINS = 4
HEAT_SWEEPS = 3
BAND = 6


def face_halos(block, sides):
    halos = []
    for axis, dim in sides:
        count = lax.axis_size(axis)
        forward = [(i, i + 1) for i in range(count - 1)]
        backward = [(i + 1, i) for i in range(count - 1)]
        size = block.shape[dim]
        low = lax.ppermute(lax.slice_in_dim(block, size - 1, size, axis=dim), axis, forward)
        high = lax.ppermute(lax.slice_in_dim(block, 0, 1, axis=dim), axis, backward)
        halos.append((low, high))
    return halos


def neighbours_of(block, halos, lead=0):
    out = []
    for k, (low, high) in enumerate(halos):
        dim = lead + k
        size = block.shape[dim]
        out.append(jnp.concatenate([lax.slice_in_dim(block, 1, size, axis=dim), high], axis=dim))
        out.append(jnp.concatenate([low, lax.slice_in_dim(block, 0, size - 1, axis=dim)], axis=dim))
    last = block.ndim - 1
    size = block.shape[last]
    zero = jnp.zeros_like(lax.slice_in_dim(block, 0, 1, axis=last))
    out.append(jnp.concatenate([lax.slice_in_dim(block, 1, size, axis=last), zero], axis=last))
    out.append(jnp.concatenate([zero, lax.slice_in_dim(block, 0, size - 1, axis=last)], axis=last))
    return out


def bernoulli(value):
    small = jnp.abs(value) < 0.0001
    return jnp.where(small, 1.0 - 0.5 * value, value / (jnp.exp(value) - 1.0))


def per_device(
    electrostatic_voltages,
    initial_electrons,
    creation_amounts,
    annihilation_coefficient,
    crystal_orientation_class,
    crystal_barrier_shift,
    restrict_matrix_first,
    restrict_matrix_second,
    restrict_matrix_third,
    cooling_coefficient,
    initial_warming,
):
    upper_limit = lax.Precision.HIGHEST
    slab_cells = electrostatic_voltages.shape[0]
    slabs = lax.axis_size("slab")
    me = lax.axis_index("slab")
    shifts = [crystal_barrier_shift[grain] for grain in range(GRAINS)]
    cls = crystal_orientation_class
    shift = jnp.where(
        cls < 2,
        jnp.where(cls == 0, shifts[0], shifts[1]),
        jnp.where(cls == 2, shifts[2], shifts[3]),
    )
    effective = electrostatic_voltages + shift
    device_sides = (("slab", 0), ("gy", 1))
    both = jnp.stack([effective, initial_electrons])
    both_halos = face_halos(both, (("slab", 1), ("gy", 2)))
    beside_both = neighbours_of(both, both_halos, lead=1)
    beside_all = [b[0] for b in beside_both]
    voltage_gradients = [leftover_portion - effective for leftover_portion in beside_all]
    bernoulli_coefficients = [bernoulli(voltage_gradient) for voltage_gradient in voltage_gradients]
    denominator_quantity = annihilation_coefficient
    for bernoulli_coefficient, voltage_gradient in zip(bernoulli_coefficients, voltage_gradients):
        denominator_quantity = denominator_quantity + (bernoulli_coefficient + voltage_gradient)

    def sweep(beside):
        fraction_top_quantity = creation_amounts
        for bernoulli_coefficient, leftover_portion in zip(bernoulli_coefficients, beside):
            fraction_top_quantity = fraction_top_quantity + bernoulli_coefficient * leftover_portion
        return fraction_top_quantity / denominator_quantity

    electron_concentration = sweep([b[1] for b in beside_both])
    electron_concentration = sweep(
        neighbours_of(electron_concentration, face_halos(electron_concentration, device_sides))
    )
    n_final = electron_concentration
    y_low, y_high = face_halos(n_final, (("gy", 1),))[0]
    zero_x = jnp.zeros_like(n_final[:1])
    beside_final = neighbours_of(n_final, [(zero_x, zero_x), (y_low, y_high)])
    joule_power_input = jnp.zeros_like(n_final)
    for bernoulli_coefficient, voltage_gradient, leftover_portion in zip(
        bernoulli_coefficients, voltage_gradients, beside_final
    ):
        joule_power_input = joule_power_input + voltage_gradient * (
            bernoulli_coefficient * leftover_portion
            - (bernoulli_coefficient + voltage_gradient) * n_final
        )
    joule_power_input = 0.5 * joule_power_input
    down_x = voltage_gradients[1][:1]
    up_x = voltage_gradients[0][-1:]
    heat_left = -0.5 * (down_x * ((bernoulli(down_x) + down_x) * n_final[:1]))
    heat_right = -0.5 * (up_x * ((bernoulli(up_x) + up_x) * n_final[-1:]))
    heat_ext = jnp.concatenate([heat_left, joule_power_input, heat_right], axis=0)

    padded_first = jnp.pad(restrict_matrix_first, ((1, 1), (1, 1)))
    ratio = slab_cells // 2
    columns_ext = lax.dynamic_slice(
        padded_first, (me * ratio, me * slab_cells), (BAND, slab_cells + 2)
    )
    columns = columns_ext[:, 1 : 1 + slab_cells]
    along_y = jnp.einsum(
        "ty,xyz->xtz", restrict_matrix_second, heat_ext, precision=upper_limit
    )
    along_z = jnp.einsum("cz,xtz->ctx", restrict_matrix_third, along_y, precision=upper_limit)
    piece = jnp.einsum("ctx,ax->cta", along_z, columns_ext, precision=upper_limit)
    chunk_c = piece.shape[0] // slabs
    piece = piece.reshape(slabs, chunk_c, piece.shape[1], BAND)
    got = lax.all_to_all(piece, "slab", 0, 0, tiled=False)
    main = got[..., 1 : 1 + ratio]
    zero_row = jnp.zeros_like(got[:1, ..., 0])
    left = jnp.concatenate([got[1:, ..., 0], zero_row], axis=0)
    right = jnp.concatenate([zero_row, got[:-1, ..., ratio + 1]], axis=0)
    main = main.at[..., ratio - 1].add(left)
    main = main.at[..., 0].add(right)
    source = jnp.transpose(main, (1, 2, 0, 3)).reshape(chunk_c, main.shape[2], slabs * ratio)

    stacked = jnp.stack([initial_warming, source, 6.0 + cooling_coefficient])
    depths = (HEAT_SWEEPS, 8)
    for (axis, dim), depth in zip((("slab", 1), ("gy", 2)), depths):
        count = lax.axis_size(axis)
        forward = [(i, i + 1) for i in range(count - 1)]
        backward = [(i + 1, i) for i in range(count - 1)]
        size = stacked.shape[dim]
        low = lax.ppermute(lax.slice_in_dim(stacked, size - depth, size, axis=dim), axis, forward)
        high = lax.ppermute(lax.slice_in_dim(stacked, 0, depth, axis=dim), axis, backward)
        stacked = jnp.concatenate([low, stacked, high], axis=dim)
    tc, tb = initial_warming.shape[0], initial_warming.shape[1]
    c_index = lax.broadcasted_iota(jnp.int32, stacked.shape[1:], 0) + (me * tc - depths[0])
    b_index = lax.broadcasted_iota(jnp.int32, stacked.shape[1:], 1) + (
        lax.axis_index("gy") * tb - depths[1]
    )
    inside = (
        (c_index >= 0)
        & (c_index < slabs * tc)
        & (b_index >= 0)
        & (b_index < lax.axis_size("gy") * tb)
    )
    warm = stacked[0]
    source_ext, scale_ext = stacked[1], stacked[2]
    for repeat in range(HEAT_SWEEPS):
        padded = jnp.pad(warm, 1)
        total = source_ext
        for leftover_portion in (
            padded[2:, 1:-1, 1:-1],
            padded[:-2, 1:-1, 1:-1],
            padded[1:-1, 2:, 1:-1],
            padded[1:-1, :-2, 1:-1],
            padded[1:-1, 1:-1, 2:],
            padded[1:-1, 1:-1, :-2],
        ):
            total = total + leftover_portion
        warm = jnp.where(inside, total / scale_ext, 0.0)
    warming_distribution = warm[depths[0] : depths[0] + tc, depths[1] : depths[1] + tb]

    a_count = warming_distribution.shape[2]
    pick = (
        lax.broadcasted_iota(jnp.int32, (slabs, BAND, a_count), 2)
        == lax.broadcasted_iota(jnp.int32, (slabs, BAND, a_count), 0) * ratio
        + lax.broadcasted_iota(jnp.int32, (slabs, BAND, a_count), 1)
        - 1
    ).astype(jnp.float32)
    windows = jnp.einsum("ska,cba->skcb", pick, warming_distribution, precision=upper_limit)
    got_warm = lax.all_to_all(windows, "slab", 0, 0, tiled=False)
    spread = jnp.einsum("skcb,kx->scbx", got_warm, columns, precision=upper_limit)
    third = restrict_matrix_third.reshape(slabs, chunk_c, restrict_matrix_third.shape[1])
    spread_y = jnp.einsum("scbx,by->scxy", spread, restrict_matrix_second, precision=upper_limit)
    fine_mesh_warming = 16.0 * jnp.einsum(
        "scxy,scz->xyz", spread_y, third, precision=upper_limit
    )
    return (electron_concentration, warming_distribution, fine_mesh_warming)


def solution(mesh):
    in_specs = (
        P("slab", "gy", None),
        P("slab", "gy", None),
        P("slab", "gy", None),
        P("slab", "gy", None),
        P("slab", "gy", None),
        P(),
        P(),
        P("gy", None),
        P(),
        P("slab", "gy", None),
        P("slab", "gy", None),
    )
    out_specs = (P("slab", "gy", None), P("slab", "gy", None), P("slab", "gy", None))
    return jax.shard_map(
        per_device, mesh=mesh, in_specs=in_specs, out_specs=out_specs, check_vma=False
    )
```
